256 devices in a mesh: member: 128 (over y, z_lo, x, core), mp: 2 (over z_hi).
Axes of the slice: x: 4, y: 4, z: 8 (z_hi: 2, z_lo: 4; z = z_hi * 4 + z_lo), core: 2. Of those that a mesh axis runs over, the one named last changes fastest.
Arguments:
- token_ids: int32 [512, 64], P('member'), may hold values from 0 to 76031
- fit_ranks: int32 [512], P('member'), may hold values from 0 to 511, as said below
- embed_table: bfloat16 [3584, 76032], P('member'), may hold values from -40 to 40
- norm_gain: float32 [3584], replicated, may hold values from 0.1 to 1.9
- qkv_weight: bfloat16 [3584, 2304], P('member', 'mp'), may hold values from -0.09375 to 0.09375
- qkv_bias: float32 [2304], P('mp'), may hold values from -3 to 3
- out_weight: bfloat16 [3584, 1792], P('member', 'mp'), may hold values from -0.125 to 0.125
- value_weight: float32 [3584], replicated, may hold values from -0.09375 to 0.09375
- qkv_left: bfloat16 [512, 3584], P('member'), may hold values from -5 to 5
- qkv_right: bfloat16 [512, 2304], P('member', 'mp'), may hold values from -5 to 5
- out_left: bfloat16 [512, 1792], P('member', 'mp'), may hold values from -5 to 5
- out_right: bfloat16 [512, 3584], P('member'), may hold values from -5 to 5
Outputs:
- values: float32 [512, 64], P(('member', 'mp'))
- qkv_grad: float32 [3584, 2304], P('member', 'mp')
- out_grad: float32 [3584, 1792], P('member', 'mp')
The draws below stay inside these ranges and needn't reach their ends.
Inputs may be any that keep to these rules, and one draw needn't show every extreme that they name: `fit_ranks`: A member's rank is the number of members whose integer fitness score is strictly lower; equal scores share a rank.
All inputs are finite; a program needn't handle non-finite values.
Results may differ from the reference program's by a relative error of at most 0.0052.
Values may be sent and summed in bfloat16 or wider, within the bound.
No kernel may reach another device: no remote copies, remote signals or barrier semaphores. Data moves between devices by JAX's collectives and lax.ppermute only.
A program may use at most 128 MiB of HBM per device.

```python
import math
import jax
import jax.numpy as jnp
import numpy as np
from jax import lax

D = 3584
HD = 128
HQ = 14
HK = 2
V = 76032
SEQ = 64
POP = 512
BLOCKS = 2
QKV = 2304
QW = 1792


def draw_fit_ranks(key, part):
    jitter = jax.random.randint(key, (POP,), 0, 64)
    upward = jnp.arange(POP, dtype=jnp.int32) * 128 // POP
    scores = jitter + upward
    lower_count = jnp.sum((scores[None, :] < scores[:, None]).astype(jnp.int32), axis=1)
    return lower_count.astype(jnp.int32)


def draw_embed_table(key, part):
    key_rows = jax.random.fold_in(key, 11)
    key_cols = jax.random.fold_in(key, 12)
    key_body = jax.random.fold_in(key, 13)
    feature_scale = jnp.exp(jax.random.uniform(key_rows, (D, 1), jnp.float32, math.log(0.3), math.log(3.0)))
    token_scale = jnp.exp(jax.random.uniform(key_cols, (1, V), jnp.float32, math.log(0.3), math.log(3.0)))
    entries = jax.random.truncated_normal(key_body, -4.0, 4.0, (D, V), jnp.float32)
    return (entries * feature_scale * token_scale).astype(jnp.bfloat16)


def plant(values, stream_key, least, high):
    place = [jax.random.randint(jax.random.fold_in(stream_key, axis), (), 0, length) for axis, length in enumerate(values.shape)]
    widest = values.shape.index(max(values.shape))
    next_to = place[:widest] + [(place[widest] + 1) % values.shape[widest]] + place[widest + 1:]
    return values.at[tuple(place)].set(least).at[tuple(next_to)].set(high)


def level_of(stream_key, extent, cuts, low, largest):
    factor_of = 1.0
    for axis_at, parts in cuts:
        draws = jax.random.uniform(jax.random.fold_in(jax.random.fold_in(stream_key, 6), axis_at), (parts,), jnp.float32, low / len(cuts), largest / len(cuts))
        factor_of = factor_of * jnp.repeat(jnp.exp(draws), extent[axis_at] // parts).reshape((-1,) + (1,) * (len(extent) - 1 - axis_at))
    return factor_of


def wide_ids(own_key, extent, count, lean):
    loads = [min(1 << octave, count + 1 - (1 << octave)) * (1 << 20) // math.isqrt((1 << octave) ** lean) + 1 for octave in range((count + 1).bit_length()) if 1 << octave <= count]
    width = 1 + sum(loads) // (1 << 30)
    listing = np.cumsum(np.array([max(1, weight // width) for weight in loads]))
    lot = jax.random.randint(jax.random.fold_in(own_key, 1), extent, 0, int(listing[len(loads) - 1]))
    start = jnp.left_shift(1, jnp.searchsorted(jnp.asarray(listing, jnp.int32), lot, side="right").astype(jnp.int32))
    rank = start - 1 + jax.random.randint(jax.random.fold_in(own_key, 4), extent, 0, 1 << 30) % jnp.minimum(start, count + 1 - start)
    return jax.random.permutation(jax.random.fold_in(own_key, 2), count)[rank].astype(jnp.int32)


def gaussian(rng, dims, scale, limit, shards=(), kind=jnp.bfloat16):
    values = jax.random.normal(rng, dims, jnp.float32) * scale
    if len(shards) > 0:
        values = level_of(rng, dims, shards, -0.22, 0.18) * values
    return jnp.clip(values, min=-limit, max=limit).astype(kind)


def setup_inputs(seed: int = 0) -> dict:
    streams_of = jax.random.split(jax.random.key(seed), 13)
    token_ids = plant(wide_ids(streams_of[0], (POP, SEQ), V, 2), jax.random.fold_in(streams_of[0], 3), 0, V - 1).astype(jnp.int32)
    fit_ranks = draw_fit_ranks(jax.random.fold_in(streams_of[12], 71), 0)
    embed_table = draw_embed_table(jax.random.fold_in(streams_of[12], 71), 0)
    norm_gain = jnp.clip(1.0 + 0.18 * jax.random.normal(streams_of[3], (D,), jnp.float32), 0.1, 1.9)
    qkv_weight = gaussian(streams_of[4], (D, QKV), D ** -0.5, 0.09375, ((0, 128), (1, 2)))
    qkv_bias = gaussian(streams_of[5], (QKV,), 0.5, 3.0, ((0, 2),), jnp.float32)
    out_weight = gaussian(streams_of[6], (D, QW), QW ** -0.5, 0.125, ((0, 128), (1, 2)))
    value_weight = gaussian(streams_of[7], (D,), D ** -0.5, 0.09375, (), jnp.float32)
    qkv_left = gaussian(streams_of[8], (POP, D), 1.0, 5.0, ((0, 128),))
    qkv_right = gaussian(streams_of[9], (POP, QKV), 1.0, 5.0, ((0, 128), (1, 2)))
    out_left = gaussian(streams_of[10], (POP, QW), 1.0, 5.0, ((0, 128), (1, 2)))
    out_right = gaussian(streams_of[11], (POP, D), 1.0, 5.0, ((0, 128),))
    return dict(token_ids=token_ids, fit_ranks=fit_ranks, embed_table=embed_table, norm_gain=norm_gain, qkv_weight=qkv_weight, qkv_bias=qkv_bias, out_weight=out_weight, value_weight=value_weight, qkv_left=qkv_left, qkv_right=qkv_right, out_left=out_left, out_right=out_right)


SIGMA = 0.01
EPSILON = 1e-06
THETA = 1000000.0
MASKED = -1e+30

def rope_tables(length, head_size):
    halfway = head_size // 2
    inverse = THETA ** (-(jnp.arange(halfway, dtype=jnp.float32) * 2.0 / head_size))
    places = jnp.arange(length, dtype=jnp.float32)
    angles = places[:, None] * inverse[None, :]
    angles = jnp.concatenate([angles, angles], axis=1)
    return (jnp.cos(angles), jnp.sin(angles))

def rotate(states, cosine, sine_table):
    halfway = states.shape[-1] // 2
    turned = jnp.concatenate([-states[..., halfway:], states[..., :halfway]], axis=-1)
    return states * cosine[:, None, :] + turned * sine_table[:, None, :]

def reference(token_ids, fit_ranks, embed_table, norm_gain, qkv_weight, qkv_bias, out_weight, value_weight, qkv_left, qkv_right, out_left, out_right):
    group_heads = HQ // BLOCKS
    group_kv = HK // BLOCKS
    shard_width = (HQ + 2 * HK) * HD // BLOCKS
    cosine, sine_table = rope_tables(SEQ, HD)
    causal = jnp.arange(SEQ)[None, :] <= jnp.arange(SEQ)[:, None]

    def one_member(packed):
        token_row, left_in, right_in, out_in, out_back = packed
        features = jnp.take(embed_table, token_row, axis=1).T.astype(jnp.float32)
        inverse_rms = lax.rsqrt(lax.optimization_barrier(jnp.mean(features * features, axis=1, keepdims=True)) + EPSILON)
        normed = (features * inverse_rms * norm_gain[None, :]).astype(jnp.bfloat16)
        projected = jnp.dot(normed, qkv_weight, preferred_element_type=jnp.float32)
        coef_in = jnp.dot(normed, left_in, preferred_element_type=jnp.float32)
        projected = projected + SIGMA * coef_in[:, None] * right_in.astype(jnp.float32)[None, :] + qkv_bias[None, :]
        projected = projected.reshape(SEQ, BLOCKS, shard_width)
        query_heads = projected[:, :, :group_heads * HD].reshape(SEQ, HQ, HD)
        key_heads = projected[:, :, group_heads * HD:(group_heads + group_kv) * HD].reshape(SEQ, HK, HD)
        value_heads = projected[:, :, (group_heads + group_kv) * HD:].reshape(SEQ, HK, HD)
        query_heads = rotate(query_heads, cosine, sine_table).astype(jnp.bfloat16)
        key_heads = rotate(key_heads, cosine, sine_table).astype(jnp.bfloat16)
        value_heads = value_heads.astype(jnp.bfloat16)
        grouped = query_heads.reshape(SEQ, HK, HQ // HK, HD).astype(jnp.float32)
        scores = jnp.einsum('skgd,tkd->kgst', grouped, key_heads.astype(jnp.float32)) / math.sqrt(HD)
        scores = jnp.where(causal, scores, MASKED)
        top = lax.optimization_barrier(jnp.max(scores, axis=-1, keepdims=True))
        weights = jnp.exp(scores - top)
        weights = (weights / lax.optimization_barrier(jnp.sum(weights, axis=-1, keepdims=True))).astype(jnp.bfloat16)
        context = jnp.einsum('kgst,tkd->skgd', weights.astype(jnp.float32), value_heads.astype(jnp.float32))
        context = context.astype(jnp.bfloat16).reshape(SEQ, HQ * HD)
        outcome = jnp.dot(context, out_weight.T, preferred_element_type=jnp.float32)
        coef_out = jnp.dot(context, out_in, preferred_element_type=jnp.float32)
        outcome = outcome + SIGMA * coef_out[:, None] * out_back.astype(jnp.float32)[None, :]
        residual = features + outcome
        inverse_out = lax.rsqrt(lax.optimization_barrier(jnp.mean(residual * residual, axis=1, keepdims=True)) + EPSILON)
        return lax.optimization_barrier(jnp.sum(residual * inverse_out * value_weight[None, :], axis=1))
    values = lax.map(one_member, (token_ids, qkv_left, qkv_right, out_left, out_right))
    population = token_ids.shape[0]
    rank_values = fit_ranks.astype(jnp.float32)
    center = jnp.sum(rank_values) / population
    spread = jnp.sum(rank_values * rank_values) / population - center * center
    fitness = (rank_values - center) * lax.rsqrt(spread + EPSILON)
    weighted_in = qkv_left.astype(jnp.float32) * fitness[:, None]
    qkv_grad = jnp.dot(weighted_in.T, qkv_right.astype(jnp.float32), precision=lax.Precision.HIGHEST) / (population * SIGMA)
    weighted_out = out_right.astype(jnp.float32) * fitness[:, None]
    out_grad = jnp.dot(weighted_out.T, out_left.astype(jnp.float32), precision=lax.Precision.HIGHEST) / (population * SIGMA)
    return (values, qkv_grad, out_grad)
```

```python
import math

import jax
import jax.numpy as jnp
from jax import lax
from jax.sharding import PartitionSpec as P

HD = 128
HQ = 14
HK = 2


SIGMA = 0.01
EPSILON = 1e-06
THETA = 1000000.0
MASKED = -1e30


def rope_tables(length, head_size):
    halfway = head_size // 2
    inverse = THETA ** (-(jnp.arange(halfway, dtype=jnp.float32) * 2.0 / head_size))
    places = jnp.arange(length, dtype=jnp.float32)
    angles = places[:, None] * inverse[None, :]
    angles = jnp.concatenate([angles, angles], axis=1)
    return (jnp.cos(angles), jnp.sin(angles))


def rotate(states, cosine, sine_table):
    halfway = states.shape[-1] // 2
    turned = jnp.concatenate([-states[..., halfway:], states[..., :halfway]], axis=-1)
    return states * cosine[None, :, None, :] + turned * sine_table[None, :, None, :]


def attend(query_heads, key_heads, value_heads, kv_count):
    members, length, head_count, head_size = query_heads.shape
    group_size = head_count // kv_count
    grouped = query_heads.reshape(members, length, kv_count, group_size, head_size)
    scores = jnp.einsum(
        "mskgd,mtkd->mkgst", grouped, key_heads, preferred_element_type=jnp.float32
    ) / math.sqrt(head_size)
    causal = jnp.arange(length)[None, :] <= jnp.arange(length)[:, None]
    scores = jnp.where(causal, scores, MASKED)
    top = jnp.max(scores, axis=-1, keepdims=True)
    weights = jnp.exp(scores - top)
    weights = (weights / jnp.sum(weights, axis=-1, keepdims=True)).astype(jnp.bfloat16)
    context = jnp.einsum(
        "mkgst,mtkd->mskgd", weights, value_heads, preferred_element_type=jnp.float32
    )
    return context.astype(jnp.bfloat16).reshape(members, length, head_count * head_size)


def on_device(
    token_ids,
    fit_ranks,
    embed_table,
    norm_gain,
    qkv_weight,
    qkv_bias,
    out_weight,
    value_weight,
    qkv_left,
    qkv_right,
    out_left,
    out_right,
):
    members, length = token_ids.shape
    row_count = members * length
    mp_size = lax.axis_size("mp")
    heads_here = HQ // mp_size
    kv_here = HK // mp_size
    population = members * lax.axis_size("member")
    contract_rows = (((0,), (0,)), ((), ()))
    contract_cols = (((1,), (1,)), ((), ()))
    member_count = lax.axis_size("member")
    packed_ids = jnp.concatenate([token_ids, fit_ranks[:, None]], axis=1)
    spread_ids = jnp.broadcast_to(packed_ids[None], (member_count,) + packed_ids.shape)
    every_ids = lax.all_to_all(spread_ids, "member", split_axis=0, concat_axis=0, tiled=True)
    all_ids = every_ids[:, :, :length].reshape(population, length)
    all_ranks = every_ids[:, :, length].reshape(population)
    feature_rows = qkv_weight.shape[0]
    qkv_cols = qkv_weight.shape[1]
    stacked = jnp.concatenate(
        [
            jnp.concatenate([qkv_weight, out_weight], axis=1),
            jnp.concatenate([qkv_right, out_left], axis=1),
        ],
        axis=0,
    )
    gathered = lax.all_gather(stacked, "member", axis=0)
    full_qkv = gathered[:, :feature_rows, :qkv_cols].reshape(-1, qkv_cols)
    full_out = gathered[:, :feature_rows, qkv_cols:].reshape(-1, out_weight.shape[1])
    right_cols = gathered[:, feature_rows:, :qkv_cols].reshape(population, qkv_cols)
    left_cols = gathered[:, feature_rows:, qkv_cols:].reshape(population, out_left.shape[1])
    picked = jnp.take(embed_table, all_ids.reshape(-1), axis=1)
    embedded = lax.all_to_all(picked, "member", split_axis=1, concat_axis=0, tiled=True)
    features = embedded.astype(jnp.float32)
    inverse_rms = lax.rsqrt(jnp.mean(features * features, axis=0, keepdims=True) + EPSILON)
    normed = (features * inverse_rms * norm_gain[:, None]).astype(jnp.bfloat16)
    base_proj = lax.dot_general(
        normed,
        full_qkv,
        contract_rows,
        preferred_element_type=jnp.float32,
    )
    normed_members = normed.reshape(normed.shape[0], members, length)
    coef_in = jnp.einsum("dms,md->ms", normed_members, qkv_left, preferred_element_type=jnp.float32)
    projected = (
        base_proj.reshape(members, length, -1)
        + SIGMA * coef_in[:, :, None] * qkv_right.astype(jnp.float32)[:, None, :]
        + qkv_bias[None, None, :]
    )
    query_width = heads_here * HD
    kv_width = kv_here * HD
    cosine, sine_table = rope_tables(length, HD)
    query_heads = rotate(
        projected[:, :, :query_width].reshape(members, length, heads_here, HD), cosine, sine_table
    ).astype(jnp.bfloat16)
    key_heads = rotate(
        projected[:, :, query_width : query_width + kv_width].reshape(members, length, kv_here, HD),
        cosine,
        sine_table,
    ).astype(jnp.bfloat16)
    value_heads = (
        projected[:, :, query_width + kv_width :]
        .reshape(members, length, kv_here, HD)
        .astype(jnp.bfloat16)
    )
    context = attend(query_heads, key_heads, value_heads, kv_here)
    coef_out = jnp.einsum("msq,mq->ms", context, out_left, preferred_element_type=jnp.float32)
    flat_context = context.reshape(row_count, query_width)
    share_rows = row_count // mp_size
    partial_out = lax.dot_general(
        flat_context,
        full_out,
        contract_cols,
        preferred_element_type=jnp.float32,
    )
    head_term = (
        partial_out.reshape(members, length, -1)
        + SIGMA * coef_out[:, :, None] * out_right.astype(jnp.float32)[:, None, :]
    )
    summed = lax.psum_scatter(
        head_term.reshape(row_count, -1), "mp", scatter_dimension=0, tiled=True
    )
    mp_index = lax.axis_index("mp")
    own_embed = lax.dynamic_slice_in_dim(embedded, mp_index * share_rows, share_rows, 1)
    residual = own_embed.T.astype(jnp.float32) + summed
    inverse_out = lax.rsqrt(jnp.mean(residual * residual, axis=1, keepdims=True) + EPSILON)
    value_rows = jnp.sum(residual * inverse_out * value_weight[None, :], axis=1).reshape(
        members // mp_size, length
    )
    rank_values = all_ranks.astype(jnp.float32)
    center = jnp.sum(rank_values) / population
    spread = jnp.sum(rank_values * rank_values) / population - center * center
    fitness = (rank_values - center) * lax.rsqrt(spread + EPSILON)
    factor_rows = jnp.concatenate(
        [
            qkv_left.reshape(members, member_count, feature_rows),
            out_right.reshape(members, member_count, feature_rows),
        ],
        axis=2,
    )
    factor_cols = lax.all_to_all(factor_rows, "member", split_axis=1, concat_axis=0, tiled=True)
    left_rows = factor_cols[:, 0, :feature_rows]
    right_rows = factor_cols[:, 0, feature_rows:]
    weighted_in = left_rows.astype(jnp.float32) * fitness[:, None]
    qkv_grad = lax.dot_general(
        weighted_in,
        right_cols.astype(jnp.float32),
        contract_rows,
        precision=lax.Precision.HIGHEST,
        preferred_element_type=jnp.float32,
    ) / (population * SIGMA)
    weighted_out = right_rows.astype(jnp.float32) * fitness[:, None]
    out_grad = lax.dot_general(
        weighted_out,
        left_cols.astype(jnp.float32),
        contract_rows,
        precision=lax.Precision.HIGHEST,
        preferred_element_type=jnp.float32,
    ) / (population * SIGMA)
    return (value_rows, qkv_grad, out_grad)


def solution(mesh):
    placed = (
        P("member", None),
        P("member"),
        P("member", None),
        P(),
        P("member", "mp"),
        P("mp"),
        P("member", "mp"),
        P(),
        P("member", None),
        P("member", "mp"),
        P("member", "mp"),
        P("member", None),
    )
    return jax.shard_map(
        on_device,
        mesh=mesh,
        in_specs=placed,
        out_specs=(P(("member", "mp"), None), P("member", "mp"), P("member", "mp")),
        check_vma=False,
    )
```

```python
import math

import jax
import jax.numpy as jnp
from jax import lax
from jax.sharding import PartitionSpec as P

HD = 128
HQ = 14
HK = 2


SIGMA = 0.01
EPSILON = 1e-06
THETA = 1000000.0
MASKED = -1e30


def rope_tables(length, head_size):
    halfway = head_size // 2
    inverse = THETA ** (-(jnp.arange(halfway, dtype=jnp.float32) * 2.0 / head_size))
    places = jnp.arange(length, dtype=jnp.float32)
    angles = places[:, None] * inverse[None, :]
    angles = jnp.concatenate([angles, angles], axis=1)
    return (jnp.cos(angles), jnp.sin(angles))


def rotate(states, cosine, sine_table):
    halfway = states.shape[-1] // 2
    turned = jnp.concatenate([-states[..., halfway:], states[..., :halfway]], axis=-1)
    return states * cosine[None, :, None, :] + turned * sine_table[None, :, None, :]


def attend(query_heads, key_heads, value_heads, kv_count):
    members, length, head_count, head_size = query_heads.shape
    group_size = head_count // kv_count
    grouped = query_heads.reshape(members, length, kv_count, group_size, head_size)
    scores = jnp.einsum(
        "mskgd,mtkd->mkgst", grouped, key_heads, preferred_element_type=jnp.float32
    ) / math.sqrt(head_size)
    causal = jnp.arange(length)[None, :] <= jnp.arange(length)[:, None]
    scores = jnp.where(causal, scores, MASKED)
    top = jnp.max(scores, axis=-1, keepdims=True)
    weights = jnp.exp(scores - top)
    weights = (weights / jnp.sum(weights, axis=-1, keepdims=True)).astype(jnp.bfloat16)
    context = jnp.einsum(
        "mkgst,mtkd->mskgd", weights, value_heads, preferred_element_type=jnp.float32
    )
    return context.astype(jnp.bfloat16).reshape(members, length, head_count * head_size)


def on_device(
    token_ids,
    fit_ranks,
    embed_table,
    norm_gain,
    qkv_weight,
    qkv_bias,
    out_weight,
    value_weight,
    qkv_left,
    qkv_right,
    out_left,
    out_right,
):
    members, length = token_ids.shape
    row_count = members * length
    mp_size = lax.axis_size("mp")
    heads_here = HQ // mp_size
    kv_here = HK // mp_size
    member_count = lax.axis_size("member")
    population = members * member_count
    feature_rows = qkv_weight.shape[0]
    qkv_cols = qkv_weight.shape[1]
    out_cols = out_weight.shape[1]
    contract_rows = (((0,), (0,)), ((), ()))
    packed_ids = jnp.concatenate([token_ids, fit_ranks[:, None]], axis=1)
    spread_ids = jnp.broadcast_to(packed_ids[None], (member_count,) + packed_ids.shape)
    every_ids = lax.all_to_all(spread_ids, "member", split_axis=0, concat_axis=0, tiled=True)
    all_ids = every_ids[:, :, :length].reshape(population, length)
    all_ranks = every_ids[:, :, length].reshape(population)
    stacked = jnp.concatenate(
        [
            jnp.concatenate([qkv_weight, out_weight], axis=1),
            jnp.concatenate([qkv_right, out_left], axis=1),
        ],
        axis=0,
    )
    gathered = lax.all_gather(stacked, "member", axis=0)
    block_qkv = gathered[:, :feature_rows, :qkv_cols]
    block_out = gathered[:, :feature_rows, qkv_cols:]
    right_cols = gathered[:, feature_rows:, :qkv_cols].reshape(population, qkv_cols)
    left_cols = gathered[:, feature_rows:, qkv_cols:].reshape(population, out_cols)
    picked = jnp.take(embed_table, all_ids.reshape(-1), axis=1)
    token_block = row_count
    factor_width = 2 * feature_rows * members
    factors = jnp.concatenate(
        [
            qkv_left.reshape(members, member_count, feature_rows),
            out_right.reshape(members, member_count, feature_rows),
        ],
        axis=2,
    )
    factors = factors.transpose(1, 0, 2).reshape(member_count, factor_width)
    factors = jnp.pad(factors, ((0, 0), (0, token_block - factor_width))).reshape(1, -1)
    combined = jnp.concatenate([picked, factors], axis=0)
    arrived = lax.all_to_all(combined, "member", split_axis=1, concat_axis=0, tiled=True)
    arrived = arrived.reshape(member_count, feature_rows + 1, token_block)
    embedded = arrived[:, :feature_rows, :]
    factor_cols = arrived[:, feature_rows, :factor_width].reshape(population, 2 * feature_rows)
    left_rows = factor_cols[:, :feature_rows]
    right_rows = factor_cols[:, feature_rows:]
    features = embedded.astype(jnp.float32)
    inverse_rms = lax.rsqrt(jnp.mean(features * features, axis=(0, 1), keepdims=True) + EPSILON)
    gain = norm_gain.reshape(member_count, feature_rows, 1)
    normed = (features * inverse_rms * gain).astype(jnp.bfloat16)
    base_proj = jnp.einsum("abt,abn->tn", normed, block_qkv, preferred_element_type=jnp.float32)
    normed_members = normed.reshape(member_count, feature_rows, members, length)
    left_blocks = qkv_left.reshape(members, member_count, feature_rows)
    coef_in = jnp.einsum(
        "abms,mab->ms", normed_members, left_blocks, preferred_element_type=jnp.float32
    )
    projected = (
        base_proj.reshape(members, length, -1)
        + SIGMA * coef_in[:, :, None] * qkv_right.astype(jnp.float32)[:, None, :]
        + qkv_bias[None, None, :]
    )
    query_width = heads_here * HD
    kv_width = kv_here * HD
    cosine, sine_table = rope_tables(length, HD)
    query_heads = rotate(
        projected[:, :, :query_width].reshape(members, length, heads_here, HD), cosine, sine_table
    ).astype(jnp.bfloat16)
    key_heads = rotate(
        projected[:, :, query_width : query_width + kv_width].reshape(members, length, kv_here, HD),
        cosine,
        sine_table,
    ).astype(jnp.bfloat16)
    value_heads = (
        projected[:, :, query_width + kv_width :]
        .reshape(members, length, kv_here, HD)
        .astype(jnp.bfloat16)
    )
    context = attend(query_heads, key_heads, value_heads, kv_here)
    coef_out = jnp.einsum("msq,mq->ms", context, out_left, preferred_element_type=jnp.float32)
    flat_context = context.reshape(row_count, query_width)
    partial_out = jnp.einsum(
        "tc,abc->abt", flat_context, block_out, preferred_element_type=jnp.float32
    )
    right_blocks = out_right.reshape(members, member_count, feature_rows).astype(jnp.float32)
    head_term = partial_out.reshape(member_count, feature_rows, members, length) + SIGMA * (
        right_blocks.transpose(1, 2, 0)[:, :, :, None] * coef_out[None, None, :, :]
    )
    share = members // mp_size
    head_term = head_term.reshape(member_count, feature_rows, mp_size, share * length)
    mp_index = lax.axis_index("mp")
    own_term = lax.dynamic_index_in_dim(head_term, mp_index, axis=2, keepdims=False)
    sent_term = lax.dynamic_index_in_dim(head_term, 1 - mp_index, axis=2, keepdims=False)
    got_term = lax.ppermute(sent_term.astype(jnp.bfloat16), "mp", perm=[(0, 1), (1, 0)])
    own_embed = lax.dynamic_index_in_dim(
        features.reshape(member_count, feature_rows, mp_size, share * length),
        mp_index,
        axis=2,
        keepdims=False,
    )
    residual = own_embed + own_term + got_term.astype(jnp.float32)
    inverse_out = lax.rsqrt(jnp.mean(residual * residual, axis=(0, 1), keepdims=True) + EPSILON)
    value_gain = value_weight.reshape(member_count, feature_rows, 1)
    value_rows = jnp.sum(residual * inverse_out * value_gain, axis=(0, 1)).reshape(share, length)
    rank_values = all_ranks.astype(jnp.float32)
    center = jnp.sum(rank_values) / population
    spread = jnp.sum(rank_values * rank_values) / population - center * center
    fitness = (rank_values - center) * lax.rsqrt(spread + EPSILON)
    weighted_in = left_rows.astype(jnp.float32) * fitness[:, None]
    qkv_grad = lax.dot_general(
        weighted_in,
        right_cols.astype(jnp.float32),
        contract_rows,
        precision=lax.Precision.HIGHEST,
        preferred_element_type=jnp.float32,
    ) / (population * SIGMA)
    weighted_out = right_rows.astype(jnp.float32) * fitness[:, None]
    out_grad = lax.dot_general(
        weighted_out,
        left_cols.astype(jnp.float32),
        contract_rows,
        precision=lax.Precision.HIGHEST,
        preferred_element_type=jnp.float32,
    ) / (population * SIGMA)
    return (value_rows, qkv_grad, out_grad)


def solution(mesh):
    placed = (
        P("member", None),
        P("member"),
        P("member", None),
        P(),
        P("member", "mp"),
        P("mp"),
        P("member", "mp"),
        P(),
        P("member", None),
        P("member", "mp"),
        P("member", "mp"),
        P("member", None),
    )
    return jax.shard_map(
        on_device,
        mesh=mesh,
        in_specs=placed,
        out_specs=(P(("member", "mp"), None), P("member", "mp"), P("member", "mp")),
        check_vma=False,
    )
```

```python
import math

import jax
import jax.numpy as jnp
from jax import lax
from jax.sharding import PartitionSpec as P

HD = 128
HQ = 14
HK = 2


SIGMA = 0.01
EPSILON = 1e-06
THETA = 1000000.0
MASKED = -1e30
MEMBER = ("y", "zl", "x", "c")


def rope_tables(length, head_size):
    halfway = head_size // 2
    inverse = THETA ** (-(jnp.arange(halfway, dtype=jnp.float32) * 2.0 / head_size))
    places = jnp.arange(length, dtype=jnp.float32)
    angles = places[:, None] * inverse[None, :]
    angles = jnp.concatenate([angles, angles], axis=1)
    return (jnp.cos(angles), jnp.sin(angles))


def rotate(states, cosine, sine_table):
    halfway = states.shape[-1] // 2
    turned = jnp.concatenate([-states[..., halfway:], states[..., :halfway]], axis=-1)
    return states * cosine[None, :, None, :] + turned * sine_table[None, :, None, :]


def attend(query_heads, key_heads, value_heads, kv_count):
    members, length, head_count, head_size = query_heads.shape
    group_size = head_count // kv_count
    grouped = query_heads.reshape(members, length, kv_count, group_size, head_size)
    scores = jnp.einsum(
        "mskgd,mtkd->mkgst", grouped, key_heads, preferred_element_type=jnp.float32
    ) / math.sqrt(head_size)
    causal = jnp.arange(length)[None, :] <= jnp.arange(length)[:, None]
    scores = jnp.where(causal, scores, MASKED)
    top = jnp.max(scores, axis=-1, keepdims=True)
    weights = jnp.exp(scores - top)
    weights = (weights / jnp.sum(weights, axis=-1, keepdims=True)).astype(jnp.bfloat16)
    context = jnp.einsum(
        "mkgst,mtkd->mskgd", weights, value_heads, preferred_element_type=jnp.float32
    )
    return context.astype(jnp.bfloat16).reshape(members, length, head_count * head_size)


def on_device(
    token_ids,
    fit_ranks,
    embed_table,
    norm_gain,
    qkv_weight,
    qkv_bias,
    out_weight,
    value_weight,
    qkv_left,
    qkv_right,
    out_left,
    out_right,
):
    members, length = token_ids.shape
    row_count = members * length
    mp_size = lax.axis_size("mp")
    heads_here = HQ // mp_size
    kv_here = HK // mp_size
    member_count = lax.axis_size(MEMBER)
    population = members * member_count
    feature_rows = qkv_weight.shape[0]
    qkv_cols = qkv_weight.shape[1]
    out_cols = out_weight.shape[1]
    contract_rows = (((0,), (0,)), ((), ()))
    packed_ids = jnp.concatenate([token_ids, fit_ranks[:, None]], axis=1)
    spread_ids = jnp.broadcast_to(packed_ids[None], (member_count,) + packed_ids.shape)
    every_ids = lax.all_to_all(spread_ids, MEMBER, split_axis=0, concat_axis=0, tiled=True)
    all_ids = every_ids[:, :, :length].reshape(population, length)
    all_ranks = every_ids[:, :, length].reshape(population)
    stacked = jnp.concatenate(
        [
            jnp.concatenate([qkv_weight, out_weight], axis=1),
            jnp.concatenate([qkv_right, out_left], axis=1),
        ],
        axis=0,
    )
    gathered = lax.all_gather(stacked, "x", axis=0)
    gathered = lax.all_gather(gathered, "zl", axis=0)
    gathered = lax.all_gather(gathered, "y", axis=0)
    gathered = lax.all_gather(gathered, "c", axis=3)
    gathered = gathered.reshape((member_count,) + stacked.shape)
    block_qkv = gathered[:, :feature_rows, :qkv_cols]
    block_out = gathered[:, :feature_rows, qkv_cols:]
    right_cols = gathered[:, feature_rows:, :qkv_cols].reshape(population, qkv_cols)
    left_cols = gathered[:, feature_rows:, qkv_cols:].reshape(population, out_cols)
    picked = jnp.take(embed_table, all_ids.reshape(-1), axis=1)
    token_block = row_count
    factor_width = 2 * feature_rows * members
    factors = jnp.concatenate(
        [
            qkv_left.reshape(members, member_count, feature_rows),
            out_right.reshape(members, member_count, feature_rows),
        ],
        axis=2,
    )
    factors = factors.transpose(1, 0, 2).reshape(member_count, factor_width)
    factors = jnp.pad(factors, ((0, 0), (0, token_block - factor_width))).reshape(1, -1)
    combined = jnp.concatenate([picked, factors], axis=0)
    arrived = lax.all_to_all(combined, MEMBER, split_axis=1, concat_axis=0, tiled=True)
    arrived = arrived.reshape(member_count, feature_rows + 1, token_block)
    embedded = arrived[:, :feature_rows, :]
    factor_cols = arrived[:, feature_rows, :factor_width].reshape(population, 2 * feature_rows)
    left_rows = factor_cols[:, :feature_rows]
    right_rows = factor_cols[:, feature_rows:]
    features = embedded.astype(jnp.float32)
    inverse_rms = lax.rsqrt(jnp.mean(features * features, axis=(0, 1), keepdims=True) + EPSILON)
    gain = norm_gain.reshape(member_count, feature_rows, 1)
    normed = (features * inverse_rms * gain).astype(jnp.bfloat16)
    base_proj = jnp.einsum("abt,abn->tn", normed, block_qkv, preferred_element_type=jnp.float32)
    normed_members = normed.reshape(member_count, feature_rows, members, length)
    left_blocks = qkv_left.reshape(members, member_count, feature_rows)
    coef_in = jnp.einsum(
        "abms,mab->ms", normed_members, left_blocks, preferred_element_type=jnp.float32
    )
    projected = (
        base_proj.reshape(members, length, -1)
        + SIGMA * coef_in[:, :, None] * qkv_right.astype(jnp.float32)[:, None, :]
        + qkv_bias[None, None, :]
    )
    query_width = heads_here * HD
    kv_width = kv_here * HD
    cosine, sine_table = rope_tables(length, HD)
    query_heads = rotate(
        projected[:, :, :query_width].reshape(members, length, heads_here, HD), cosine, sine_table
    ).astype(jnp.bfloat16)
    key_heads = rotate(
        projected[:, :, query_width : query_width + kv_width].reshape(members, length, kv_here, HD),
        cosine,
        sine_table,
    ).astype(jnp.bfloat16)
    value_heads = (
        projected[:, :, query_width + kv_width :]
        .reshape(members, length, kv_here, HD)
        .astype(jnp.bfloat16)
    )
    context = attend(query_heads, key_heads, value_heads, kv_here)
    coef_out = jnp.einsum("msq,mq->ms", context, out_left, preferred_element_type=jnp.float32)
    flat_context = context.reshape(row_count, query_width)
    partial_out = jnp.einsum(
        "tc,abc->abt", flat_context, block_out, preferred_element_type=jnp.float32
    )
    right_blocks = out_right.reshape(members, member_count, feature_rows).astype(jnp.float32)
    head_term = partial_out.reshape(member_count, feature_rows, members, length) + SIGMA * (
        right_blocks.transpose(1, 2, 0)[:, :, :, None] * coef_out[None, None, :, :]
    )
    share = members // mp_size
    head_term = head_term.reshape(member_count, feature_rows, mp_size, share * length)
    mp_index = lax.axis_index("mp")
    own_term = lax.dynamic_index_in_dim(head_term, mp_index, axis=2, keepdims=False)
    sent_term = lax.dynamic_index_in_dim(head_term, 1 - mp_index, axis=2, keepdims=False)
    got_term = lax.ppermute(sent_term.astype(jnp.bfloat16), "mp", perm=[(0, 1), (1, 0)])
    own_embed = lax.dynamic_index_in_dim(
        features.reshape(member_count, feature_rows, mp_size, share * length),
        mp_index,
        axis=2,
        keepdims=False,
    )
    residual = own_embed + own_term + got_term.astype(jnp.float32)
    inverse_out = lax.rsqrt(jnp.mean(residual * residual, axis=(0, 1), keepdims=True) + EPSILON)
    value_gain = value_weight.reshape(member_count, feature_rows, 1)
    value_rows = jnp.sum(residual * inverse_out * value_gain, axis=(0, 1)).reshape(share, length)
    rank_values = all_ranks.astype(jnp.float32)
    center = jnp.sum(rank_values) / population
    spread = jnp.sum(rank_values * rank_values) / population - center * center
    fitness = (rank_values - center) * lax.rsqrt(spread + EPSILON)
    weighted_in = left_rows.astype(jnp.float32) * fitness[:, None]
    qkv_grad = lax.dot_general(
        weighted_in,
        right_cols.astype(jnp.float32),
        contract_rows,
        precision=lax.Precision.HIGHEST,
        preferred_element_type=jnp.float32,
    ) / (population * SIGMA)
    weighted_out = right_rows.astype(jnp.float32) * fitness[:, None]
    out_grad = lax.dot_general(
        weighted_out,
        left_cols.astype(jnp.float32),
        contract_rows,
        precision=lax.Precision.HIGHEST,
        preferred_element_type=jnp.float32,
    ) / (population * SIGMA)
    return (value_rows, qkv_grad, out_grad)


def solution(mesh):
    member_size, mp_size = mesh.devices.shape
    chips = member_size // (2 * 4 * 4)
    split_mesh = jax.sharding.Mesh(
        mesh.devices.reshape(chips, 4, 4, 2, mp_size), ("y", "zl", "x", "c", "mp")
    )
    placed = (
        P(MEMBER, None),
        P(MEMBER),
        P(MEMBER, None),
        P(),
        P(MEMBER, "mp"),
        P("mp"),
        P(MEMBER, "mp"),
        P(),
        P(MEMBER, None),
        P(MEMBER, "mp"),
        P(MEMBER, "mp"),
        P(MEMBER, None),
    )
    return jax.shard_map(
        on_device,
        mesh=split_mesh,
        in_specs=placed,
        out_specs=(P(MEMBER + ("mp",), None), P(MEMBER, "mp"), P(MEMBER, "mp")),
        check_vma=False,
    )
```

```python
import math

import jax
import jax.numpy as jnp
from jax import lax
from jax.sharding import PartitionSpec as P

HD = 128
HQ = 14
HK = 2


SIGMA = 0.01
EPSILON = 1e-06
THETA = 1000000.0
MASKED = -1e30
MEMBER = ("y", "zl", "x", "c")
CHIP_AXES = ("y", "zl", "x")


def rope_tables(length, head_size):
    halfway = head_size // 2
    inverse = THETA ** (-(jnp.arange(halfway, dtype=jnp.float32) * 2.0 / head_size))
    places = jnp.arange(length, dtype=jnp.float32)
    angles = places[:, None] * inverse[None, :]
    angles = jnp.concatenate([angles, angles], axis=1)
    return (jnp.cos(angles), jnp.sin(angles))


def rotate(states, cosine, sine_table):
    halfway = states.shape[-1] // 2
    turned = jnp.concatenate([-states[..., halfway:], states[..., :halfway]], axis=-1)
    return states * cosine[None, :, None, :] + turned * sine_table[None, :, None, :]


def attend(query_heads, key_heads, value_heads, kv_count):
    members, length, head_count, head_size = query_heads.shape
    group_size = head_count // kv_count
    grouped = query_heads.reshape(members, length, kv_count, group_size, head_size)
    scores = jnp.einsum(
        "mskgd,mtkd->mkgst", grouped, key_heads, preferred_element_type=jnp.float32
    ) / math.sqrt(head_size)
    causal = jnp.arange(length)[None, :] <= jnp.arange(length)[:, None]
    scores = jnp.where(causal, scores, MASKED)
    top = jnp.max(scores, axis=-1, keepdims=True)
    weights = jnp.exp(scores - top)
    weights = (weights / jnp.sum(weights, axis=-1, keepdims=True)).astype(jnp.bfloat16)
    context = jnp.einsum(
        "mkgst,mtkd->mskgd", weights, value_heads, preferred_element_type=jnp.float32
    )
    return context.astype(jnp.bfloat16).reshape(members, length, head_count * head_size)


def on_device(
    token_ids,
    fit_ranks,
    embed_table,
    norm_gain,
    qkv_weight,
    qkv_bias,
    out_weight,
    value_weight,
    qkv_left,
    qkv_right,
    out_left,
    out_right,
):
    members, length = token_ids.shape
    row_count = members * length
    mp_size = lax.axis_size("mp")
    heads_here = HQ // mp_size
    kv_here = HK // mp_size
    member_count = lax.axis_size(MEMBER)
    population = members * member_count
    feature_rows = qkv_weight.shape[0]
    qkv_cols = qkv_weight.shape[1]
    out_cols = out_weight.shape[1]
    contract_rows = (((0,), (0,)), ((), ()))
    packed_ids = jnp.concatenate([token_ids, fit_ranks[:, None]], axis=1)
    spread_ids = jnp.broadcast_to(packed_ids[None], (member_count,) + packed_ids.shape)
    every_ids = lax.all_to_all(spread_ids, MEMBER, split_axis=0, concat_axis=0, tiled=True)
    all_ids = every_ids[:, :, :length].reshape(population, length)
    all_ranks = every_ids[:, :, length].reshape(population)
    stacked = jnp.concatenate(
        [
            jnp.concatenate([qkv_weight, out_weight], axis=1),
            jnp.concatenate([qkv_right, out_left], axis=1),
        ],
        axis=0,
    )
    chip_gathered = lax.all_gather(stacked, CHIP_AXES, axis=0)
    picked = jnp.take(embed_table, all_ids.reshape(-1), axis=1)
    after_pick = picked[0, 0] * jnp.zeros((), picked.dtype)
    gathered = lax.all_gather(chip_gathered + after_pick, "c", axis=1)
    gathered = gathered.reshape((member_count,) + stacked.shape)
    block_qkv = gathered[:, :feature_rows, :qkv_cols]
    block_out = gathered[:, :feature_rows, qkv_cols:]
    right_cols = gathered[:, feature_rows:, :qkv_cols].reshape(population, qkv_cols)
    left_cols = gathered[:, feature_rows:, qkv_cols:].reshape(population, out_cols)
    token_block = row_count
    factor_width = 2 * feature_rows * members
    factors = jnp.concatenate(
        [
            qkv_left.reshape(members, member_count, feature_rows),
            out_right.reshape(members, member_count, feature_rows),
        ],
        axis=2,
    )
    factors = factors.transpose(1, 0, 2).reshape(member_count, factor_width)
    factors = jnp.pad(factors, ((0, 0), (0, token_block - factor_width))).reshape(1, -1)
    combined = jnp.concatenate([picked, factors], axis=0)
    arrived = lax.all_to_all(combined, MEMBER, split_axis=1, concat_axis=0, tiled=True)
    arrived = arrived.reshape(member_count, feature_rows + 1, token_block)
    embedded = arrived[:, :feature_rows, :]
    factor_cols = arrived[:, feature_rows, :factor_width].reshape(population, 2 * feature_rows)
    left_rows = factor_cols[:, :feature_rows]
    right_rows = factor_cols[:, feature_rows:]
    features = embedded.astype(jnp.float32)
    inverse_rms = lax.rsqrt(jnp.mean(features * features, axis=(0, 1), keepdims=True) + EPSILON)
    gain = norm_gain.reshape(member_count, feature_rows, 1)
    normed = (features * inverse_rms * gain).astype(jnp.bfloat16)
    base_proj = jnp.einsum("abt,abn->tn", normed, block_qkv, preferred_element_type=jnp.float32)
    normed_members = normed.reshape(member_count, feature_rows, members, length)
    left_blocks = qkv_left.reshape(members, member_count, feature_rows)
    coef_in = jnp.einsum(
        "abms,mab->ms", normed_members, left_blocks, preferred_element_type=jnp.float32
    )
    projected = (
        base_proj.reshape(members, length, -1)
        + SIGMA * coef_in[:, :, None] * qkv_right.astype(jnp.float32)[:, None, :]
        + qkv_bias[None, None, :]
    )
    query_width = heads_here * HD
    kv_width = kv_here * HD
    cosine, sine_table = rope_tables(length, HD)
    query_heads = rotate(
        projected[:, :, :query_width].reshape(members, length, heads_here, HD), cosine, sine_table
    ).astype(jnp.bfloat16)
    key_heads = rotate(
        projected[:, :, query_width : query_width + kv_width].reshape(members, length, kv_here, HD),
        cosine,
        sine_table,
    ).astype(jnp.bfloat16)
    value_heads = (
        projected[:, :, query_width + kv_width :]
        .reshape(members, length, kv_here, HD)
        .astype(jnp.bfloat16)
    )
    context = attend(query_heads, key_heads, value_heads, kv_here)
    coef_out = jnp.einsum("msq,mq->ms", context, out_left, preferred_element_type=jnp.float32)
    flat_context = context.reshape(row_count, query_width)
    partial_out = jnp.einsum(
        "tc,abc->abt", flat_context, block_out, preferred_element_type=jnp.float32
    )
    right_blocks = out_right.reshape(members, member_count, feature_rows).astype(jnp.float32)
    head_term = partial_out.reshape(member_count, feature_rows, members, length) + SIGMA * (
        right_blocks.transpose(1, 2, 0)[:, :, :, None] * coef_out[None, None, :, :]
    )
    share = members // mp_size
    head_term = head_term.reshape(member_count, feature_rows, mp_size, share * length)
    mp_index = lax.axis_index("mp")
    own_term = lax.dynamic_index_in_dim(head_term, mp_index, axis=2, keepdims=False)
    sent_term = lax.dynamic_index_in_dim(head_term, 1 - mp_index, axis=2, keepdims=False)
    got_term = lax.ppermute(sent_term.astype(jnp.bfloat16), "mp", perm=[(0, 1), (1, 0)])
    own_embed = lax.dynamic_index_in_dim(
        features.reshape(member_count, feature_rows, mp_size, share * length),
        mp_index,
        axis=2,
        keepdims=False,
    )
    residual = own_embed + own_term + got_term.astype(jnp.float32)
    inverse_out = lax.rsqrt(jnp.mean(residual * residual, axis=(0, 1), keepdims=True) + EPSILON)
    value_gain = value_weight.reshape(member_count, feature_rows, 1)
    value_rows = jnp.sum(residual * inverse_out * value_gain, axis=(0, 1)).reshape(share, length)
    rank_values = all_ranks.astype(jnp.float32)
    center = jnp.sum(rank_values) / population
    spread = jnp.sum(rank_values * rank_values) / population - center * center
    fitness = (rank_values - center) * lax.rsqrt(spread + EPSILON)
    weighted_in = left_rows.astype(jnp.float32) * fitness[:, None]
    qkv_grad = lax.dot_general(
        weighted_in,
        right_cols.astype(jnp.float32),
        contract_rows,
        precision=lax.Precision.HIGHEST,
        preferred_element_type=jnp.float32,
    ) / (population * SIGMA)
    weighted_out = right_rows.astype(jnp.float32) * fitness[:, None]
    out_grad = lax.dot_general(
        weighted_out,
        left_cols.astype(jnp.float32),
        contract_rows,
        precision=lax.Precision.HIGHEST,
        preferred_element_type=jnp.float32,
    ) / (population * SIGMA)
    return (value_rows, qkv_grad, out_grad)


def solution(mesh):
    member_size, mp_size = mesh.devices.shape
    chips = member_size // (2 * 4 * 4)
    split_mesh = jax.sharding.Mesh(
        mesh.devices.reshape(chips, 4, 4, 2, mp_size), ("y", "zl", "x", "c", "mp")
    )
    placed = (
        P(MEMBER, None),
        P(MEMBER),
        P(MEMBER, None),
        P(),
        P(MEMBER, "mp"),
        P("mp"),
        P(MEMBER, "mp"),
        P(),
        P(MEMBER, None),
        P(MEMBER, "mp"),
        P(MEMBER, "mp"),
        P(MEMBER, None),
    )
    return jax.shard_map(
        on_device,
        mesh=split_mesh,
        in_specs=placed,
        out_specs=(P(MEMBER + ("mp",), None), P(MEMBER, "mp"), P(MEMBER, "mp")),
        check_vma=False,
    )
```

```python
import math

import jax
import jax.numpy as jnp
from jax import lax
from jax.sharding import PartitionSpec as P

HD = 128
HQ = 14
HK = 2


SIGMA = 0.01
EPSILON = 1e-06
THETA = 1000000.0
MASKED = -1e30


def rope_tables(length, head_size):
    halfway = head_size // 2
    inverse = THETA ** (-(jnp.arange(halfway, dtype=jnp.float32) * 2.0 / head_size))
    places = jnp.arange(length, dtype=jnp.float32)
    angles = places[:, None] * inverse[None, :]
    angles = jnp.concatenate([angles, angles], axis=1)
    return (jnp.cos(angles), jnp.sin(angles))


def rotate(states, cosine, sine_table):
    halfway = states.shape[-1] // 2
    turned = jnp.concatenate([-states[..., halfway:], states[..., :halfway]], axis=-1)
    return states * cosine[None, :, None, :] + turned * sine_table[None, :, None, :]


def attend(query_heads, key_heads, value_heads, kv_count):
    members, length, head_count, head_size = query_heads.shape
    group_size = head_count // kv_count
    grouped = query_heads.reshape(members, length, kv_count, group_size, head_size)
    scores = jnp.einsum(
        "mskgd,mtkd->mkgst", grouped, key_heads, preferred_element_type=jnp.float32
    ) / math.sqrt(head_size)
    causal = jnp.arange(length)[None, :] <= jnp.arange(length)[:, None]
    scores = jnp.where(causal, scores, MASKED)
    top = jnp.max(scores, axis=-1, keepdims=True)
    weights = jnp.exp(scores - top)
    weights = (weights / jnp.sum(weights, axis=-1, keepdims=True)).astype(jnp.bfloat16)
    context = jnp.einsum(
        "mkgst,mtkd->mskgd", weights, value_heads, preferred_element_type=jnp.float32
    )
    return context.astype(jnp.bfloat16).reshape(members, length, head_count * head_size)


def on_device(
    token_ids,
    fit_ranks,
    embed_table,
    norm_gain,
    qkv_weight,
    qkv_bias,
    out_weight,
    value_weight,
    qkv_left,
    qkv_right,
    out_left,
    out_right,
):
    members, length = token_ids.shape
    row_count = members * length
    mp_size = lax.axis_size("mp")
    heads_here = HQ // mp_size
    kv_here = HK // mp_size
    member_count = lax.axis_size("member")
    population = members * member_count
    feature_rows = qkv_weight.shape[0]
    qkv_cols = qkv_weight.shape[1]
    out_cols = out_weight.shape[1]
    contract_rows = (((0,), (0,)), ((), ()))
    packed_ids = jnp.concatenate([token_ids, fit_ranks[:, None]], axis=1)
    spread_ids = jnp.broadcast_to(packed_ids[None], (member_count,) + packed_ids.shape)
    every_ids = lax.all_to_all(spread_ids, "member", split_axis=0, concat_axis=0, tiled=True)
    all_ids = every_ids[:, :, :length].reshape(population, length)
    all_ranks = every_ids[:, :, length].reshape(population)
    stacked = jnp.concatenate(
        [
            jnp.concatenate([qkv_weight, out_weight], axis=1),
            jnp.concatenate([qkv_right, out_left], axis=1),
        ],
        axis=0,
    )
    gathered = lax.all_gather(stacked, "member", axis=0)
    block_rows = gathered.shape[1]
    block_qkv = gathered[:, :, :qkv_cols]
    block_out = gathered[:, :, qkv_cols:]
    right_cols = gathered[:, feature_rows:, :qkv_cols].reshape(population, qkv_cols)
    left_cols = gathered[:, feature_rows:, qkv_cols:].reshape(population, out_cols)
    picked = jnp.take(embed_table, all_ids.reshape(-1), axis=1)
    token_block = row_count
    factor_width = 2 * feature_rows * members
    factors = jnp.concatenate(
        [
            qkv_left.reshape(members, member_count, feature_rows),
            out_right.reshape(members, member_count, feature_rows),
        ],
        axis=2,
    )
    factors = factors.transpose(1, 0, 2).reshape(member_count, factor_width)
    factors = jnp.pad(factors, ((0, 0), (0, token_block - factor_width))).reshape(1, -1)
    spare = jnp.zeros((block_rows - feature_rows - 1, picked.shape[1]), picked.dtype)
    combined = jnp.concatenate([picked, factors, spare], axis=0)
    arrived = lax.all_to_all(combined, "member", split_axis=1, concat_axis=0, tiled=True)
    arrived = arrived.reshape(member_count, block_rows, token_block)
    factor_cols = arrived[:, feature_rows, :factor_width].reshape(population, 2 * feature_rows)
    real_row = (jnp.arange(block_rows) < feature_rows)[None, :, None]
    left_rows = factor_cols[:, :feature_rows]
    right_rows = factor_cols[:, feature_rows:]
    feature_count = member_count * feature_rows
    features = jnp.where(real_row, arrived.astype(jnp.float32), 0.0)
    inverse_rms = lax.rsqrt(
        jnp.sum(features * features, axis=(0, 1), keepdims=True) / feature_count + EPSILON
    )
    row_pad = ((0, 0), (0, block_rows - feature_rows))
    gain = jnp.pad(norm_gain.reshape(member_count, feature_rows), row_pad)[:, :, None]
    normed = (features * inverse_rms * gain).astype(jnp.bfloat16)
    base_proj = jnp.einsum("abt,abn->tn", normed, block_qkv, preferred_element_type=jnp.float32)
    normed_members = normed.reshape(member_count, block_rows, members, length)
    left_blocks = jnp.pad(
        qkv_left.reshape(members, member_count, feature_rows), ((0, 0),) + row_pad
    )
    coef_in = jnp.einsum(
        "abms,mab->ms", normed_members, left_blocks, preferred_element_type=jnp.float32
    )
    projected = (
        base_proj.reshape(members, length, -1)
        + SIGMA * coef_in[:, :, None] * qkv_right.astype(jnp.float32)[:, None, :]
        + qkv_bias[None, None, :]
    )
    query_width = heads_here * HD
    kv_width = kv_here * HD
    cosine, sine_table = rope_tables(length, HD)
    query_heads = rotate(
        projected[:, :, :query_width].reshape(members, length, heads_here, HD), cosine, sine_table
    ).astype(jnp.bfloat16)
    key_heads = rotate(
        projected[:, :, query_width : query_width + kv_width].reshape(members, length, kv_here, HD),
        cosine,
        sine_table,
    ).astype(jnp.bfloat16)
    value_heads = (
        projected[:, :, query_width + kv_width :]
        .reshape(members, length, kv_here, HD)
        .astype(jnp.bfloat16)
    )
    context = attend(query_heads, key_heads, value_heads, kv_here)
    coef_out = jnp.einsum("msq,mq->ms", context, out_left, preferred_element_type=jnp.float32)
    flat_context = context.reshape(row_count, query_width)
    partial_out = jnp.einsum(
        "tc,abc->abt", flat_context, block_out, preferred_element_type=jnp.float32
    )
    right_blocks = out_right.reshape(members, member_count, feature_rows).astype(jnp.float32)
    head_term = partial_out[:, :feature_rows].reshape(
        member_count, feature_rows, members, length
    ) + SIGMA * (right_blocks.transpose(1, 2, 0)[:, :, :, None] * coef_out[None, None, :, :])
    share = members // mp_size
    head_term = head_term.reshape(member_count, feature_rows, mp_size, share * length)
    mp_index = lax.axis_index("mp")
    own_term = lax.dynamic_index_in_dim(head_term, mp_index, axis=2, keepdims=False)
    sent_term = lax.dynamic_index_in_dim(head_term, 1 - mp_index, axis=2, keepdims=False)
    got_term = lax.ppermute(sent_term.astype(jnp.bfloat16), "mp", perm=[(0, 1), (1, 0)])
    own_embed = lax.dynamic_index_in_dim(
        features[:, :feature_rows].reshape(member_count, feature_rows, mp_size, share * length),
        mp_index,
        axis=2,
        keepdims=False,
    )
    residual = own_embed + own_term + got_term.astype(jnp.float32)
    inverse_out = lax.rsqrt(jnp.mean(residual * residual, axis=(0, 1), keepdims=True) + EPSILON)
    value_gain = value_weight.reshape(member_count, feature_rows, 1)
    value_rows = jnp.sum(residual * inverse_out * value_gain, axis=(0, 1)).reshape(share, length)
    rank_values = all_ranks.astype(jnp.float32)
    center = jnp.sum(rank_values) / population
    spread = jnp.sum(rank_values * rank_values) / population - center * center
    fitness = (rank_values - center) * lax.rsqrt(spread + EPSILON)
    weighted_in = left_rows.astype(jnp.float32) * fitness[:, None]
    qkv_grad = lax.dot_general(
        weighted_in,
        right_cols.astype(jnp.float32),
        contract_rows,
        precision=lax.Precision.HIGHEST,
        preferred_element_type=jnp.float32,
    ) / (population * SIGMA)
    weighted_out = right_rows.astype(jnp.float32) * fitness[:, None]
    out_grad = lax.dot_general(
        weighted_out,
        left_cols.astype(jnp.float32),
        contract_rows,
        precision=lax.Precision.HIGHEST,
        preferred_element_type=jnp.float32,
    ) / (population * SIGMA)
    return (value_rows, qkv_grad, out_grad)


def solution(mesh):
    placed = (
        P("member", None),
        P("member"),
        P("member", None),
        P(),
        P("member", "mp"),
        P("mp"),
        P("member", "mp"),
        P(),
        P("member", None),
        P("member", "mp"),
        P("member", "mp"),
        P("member", None),
    )
    return jax.shard_map(
        on_device,
        mesh=mesh,
        in_specs=placed,
        out_specs=(P(("member", "mp"), None), P("member", "mp"), P("member", "mp")),
        check_vma=False,
    )
```

```python
import math

import jax
import numpy as np
import jax.numpy as jnp
from jax import lax
from jax.sharding import PartitionSpec as P

HD = 128
HQ = 14
HK = 2


SIGMA = 0.01
EPSILON = 1e-06
THETA = 1000000.0
MASKED = -1e30


def rope_tables(length, head_size):
    halfway = head_size // 2
    steps = np.arange(halfway, dtype=np.float32) * np.float32(2.0) / np.float32(head_size)
    inverse = np.power(np.float32(THETA), -steps).astype(np.float32)
    places = np.arange(length, dtype=np.float32)
    angles = (places[:, None] * inverse[None, :]).astype(np.float32)
    angles = np.concatenate([angles, angles], axis=1).astype(np.float64)
    cosine = np.cos(angles).astype(np.float32)
    sine_table = np.sin(angles).astype(np.float32)
    return (jnp.asarray(cosine), jnp.asarray(sine_table))


def rotate(states, cosine, sine_table):
    halfway = states.shape[-1] // 2
    turned = jnp.concatenate([-states[..., halfway:], states[..., :halfway]], axis=-1)
    return states * cosine[None, :, None, :] + turned * sine_table[None, :, None, :]


def attend(query_heads, key_heads, value_heads, kv_count):
    members, length, head_count, head_size = query_heads.shape
    group_size = head_count // kv_count
    grouped = query_heads.reshape(members, length, kv_count, group_size, head_size)
    scores = jnp.einsum(
        "mskgd,mtkd->mkgst", grouped, key_heads, preferred_element_type=jnp.float32
    ) / math.sqrt(head_size)
    causal = jnp.arange(length)[None, :] <= jnp.arange(length)[:, None]
    scores = jnp.where(causal, scores, MASKED)
    top = jnp.max(scores, axis=-1, keepdims=True)
    weights = jnp.exp(scores - top)
    weights = (weights / jnp.sum(weights, axis=-1, keepdims=True)).astype(jnp.bfloat16)
    context = jnp.einsum(
        "mkgst,mtkd->mskgd", weights, value_heads, preferred_element_type=jnp.float32
    )
    return context.astype(jnp.bfloat16).reshape(members, length, head_count * head_size)


def on_device(
    token_ids,
    fit_ranks,
    embed_table,
    norm_gain,
    qkv_weight,
    qkv_bias,
    out_weight,
    value_weight,
    qkv_left,
    qkv_right,
    out_left,
    out_right,
):
    members, length = token_ids.shape
    row_count = members * length
    mp_size = lax.axis_size("mp")
    heads_here = HQ // mp_size
    kv_here = HK // mp_size
    member_count = lax.axis_size("member")
    population = members * member_count
    feature_rows = qkv_weight.shape[0]
    qkv_cols = qkv_weight.shape[1]
    out_cols = out_weight.shape[1]
    contract_rows = (((0,), (0,)), ((), ()))
    packed_ids = jnp.concatenate([token_ids, fit_ranks[:, None]], axis=1)
    spread_ids = jnp.broadcast_to(packed_ids[None], (member_count,) + packed_ids.shape)
    every_ids = lax.all_to_all(spread_ids, "member", split_axis=0, concat_axis=0, tiled=True)
    all_ids = every_ids[:, :, :length].reshape(population, length)
    all_ranks = every_ids[:, :, length].reshape(population)
    stacked = jnp.concatenate(
        [
            jnp.concatenate([qkv_weight, out_weight], axis=1),
            jnp.concatenate([qkv_right, out_left], axis=1),
        ],
        axis=0,
    )
    gathered = lax.all_gather(stacked, "member", axis=0)
    block_qkv = gathered[:, :feature_rows, :qkv_cols]
    block_out = gathered[:, :feature_rows, qkv_cols:]
    right_cols = gathered[:, feature_rows:, :qkv_cols].reshape(population, qkv_cols)
    left_cols = gathered[:, feature_rows:, qkv_cols:].reshape(population, out_cols)
    picked = embed_table.at[:, all_ids.reshape(-1)].get(mode="promise_in_bounds")
    token_block = row_count
    factor_width = 2 * feature_rows * members
    factors = jnp.concatenate(
        [
            qkv_left.reshape(members, member_count, feature_rows),
            out_right.reshape(members, member_count, feature_rows),
        ],
        axis=2,
    )
    factors = factors.transpose(1, 0, 2).reshape(member_count, factor_width)
    factors = jnp.pad(factors, ((0, 0), (0, token_block - factor_width))).reshape(1, -1)
    combined = jnp.concatenate([picked, factors], axis=0)
    arrived = lax.all_to_all(combined, "member", split_axis=1, concat_axis=0, tiled=True)
    arrived = arrived.reshape(member_count, feature_rows + 1, token_block)
    embedded = arrived[:, :feature_rows, :]
    factor_cols = arrived[:, feature_rows, :factor_width].reshape(population, 2 * feature_rows)
    left_rows = factor_cols[:, :feature_rows]
    right_rows = factor_cols[:, feature_rows:]
    features = embedded.astype(jnp.float32)
    inverse_rms = lax.rsqrt(jnp.mean(features * features, axis=(0, 1), keepdims=True) + EPSILON)
    gain = norm_gain.reshape(member_count, feature_rows, 1)
    normed = (features * inverse_rms * gain).astype(jnp.bfloat16)
    base_proj = jnp.einsum("abt,abn->tn", normed, block_qkv, preferred_element_type=jnp.float32)
    normed_members = normed.reshape(member_count, feature_rows, members, length)
    left_blocks = qkv_left.reshape(members, member_count, feature_rows)
    coef_in = jnp.einsum(
        "abms,mab->ms", normed_members, left_blocks, preferred_element_type=jnp.float32
    )
    projected = (
        base_proj.reshape(members, length, -1)
        + SIGMA * coef_in[:, :, None] * qkv_right.astype(jnp.float32)[:, None, :]
        + qkv_bias[None, None, :]
    )
    query_width = heads_here * HD
    kv_width = kv_here * HD
    cosine, sine_table = rope_tables(length, HD)
    query_heads = rotate(
        projected[:, :, :query_width].reshape(members, length, heads_here, HD), cosine, sine_table
    ).astype(jnp.bfloat16)
    key_heads = rotate(
        projected[:, :, query_width : query_width + kv_width].reshape(members, length, kv_here, HD),
        cosine,
        sine_table,
    ).astype(jnp.bfloat16)
    value_heads = (
        projected[:, :, query_width + kv_width :]
        .reshape(members, length, kv_here, HD)
        .astype(jnp.bfloat16)
    )
    context = attend(query_heads, key_heads, value_heads, kv_here)
    coef_out = jnp.einsum("msq,mq->ms", context, out_left, preferred_element_type=jnp.float32)
    flat_context = context.reshape(row_count, query_width)
    partial_out = jnp.einsum(
        "tc,abc->abt", flat_context, block_out, preferred_element_type=jnp.float32
    )
    right_blocks = out_right.reshape(members, member_count, feature_rows).astype(jnp.float32)
    head_term = partial_out.reshape(member_count, feature_rows, members, length) + SIGMA * (
        right_blocks.transpose(1, 2, 0)[:, :, :, None] * coef_out[None, None, :, :]
    )
    share = members // mp_size
    head_term = head_term.reshape(member_count, feature_rows, mp_size, share * length)
    mp_index = lax.axis_index("mp")
    own_term = lax.dynamic_index_in_dim(head_term, mp_index, axis=2, keepdims=False)
    sent_term = lax.dynamic_index_in_dim(head_term, 1 - mp_index, axis=2, keepdims=False)
    got_term = lax.ppermute(sent_term.astype(jnp.bfloat16), "mp", perm=[(0, 1), (1, 0)])
    own_embed = lax.dynamic_index_in_dim(
        features.reshape(member_count, feature_rows, mp_size, share * length),
        mp_index,
        axis=2,
        keepdims=False,
    )
    residual = own_embed + own_term + got_term.astype(jnp.float32)
    inverse_out = lax.rsqrt(jnp.mean(residual * residual, axis=(0, 1), keepdims=True) + EPSILON)
    value_gain = value_weight.reshape(member_count, feature_rows, 1)
    value_rows = jnp.sum(residual * inverse_out * value_gain, axis=(0, 1)).reshape(share, length)
    rank_values = all_ranks.astype(jnp.float32)
    center = jnp.sum(rank_values) / population
    spread = jnp.sum(rank_values * rank_values) / population - center * center
    fitness = (rank_values - center) * lax.rsqrt(spread + EPSILON)
    weighted_in = left_rows.astype(jnp.float32) * fitness[:, None]
    qkv_grad = lax.dot_general(
        weighted_in,
        right_cols.astype(jnp.float32),
        contract_rows,
        precision=lax.Precision.HIGHEST,
        preferred_element_type=jnp.float32,
    ) / (population * SIGMA)
    weighted_out = right_rows.astype(jnp.float32) * fitness[:, None]
    out_grad = lax.dot_general(
        weighted_out,
        left_cols.astype(jnp.float32),
        contract_rows,
        precision=lax.Precision.HIGHEST,
        preferred_element_type=jnp.float32,
    ) / (population * SIGMA)
    return (value_rows, qkv_grad, out_grad)


def solution(mesh):
    placed = (
        P("member", None),
        P("member"),
        P("member", None),
        P(),
        P("member", "mp"),
        P("mp"),
        P("member", "mp"),
        P(),
        P("member", None),
        P("member", "mp"),
        P("member", "mp"),
        P("member", None),
    )
    return jax.shard_map(
        on_device,
        mesh=mesh,
        in_specs=placed,
        out_specs=(P(("member", "mp"), None), P("member", "mp"), P("member", "mp")),
        check_vma=False,
    )
```

```python
import math

import jax
import numpy as np
import jax.numpy as jnp
from jax import lax
from jax.sharding import PartitionSpec as P

HD = 128
HQ = 14
HK = 2


SIGMA = 0.01
EPSILON = 1e-06
THETA = 1000000.0
MASKED = -1e30
MEMBER = ("y", "zl", "x", "c")
BLOCK_AXES = ("zl", "x", "c")


def rope_tables(length, head_size):
    halfway = head_size // 2
    steps = np.arange(halfway, dtype=np.float32) * np.float32(2.0) / np.float32(head_size)
    inverse = np.power(np.float32(THETA), -steps).astype(np.float32)
    places = np.arange(length, dtype=np.float32)
    angles = (places[:, None] * inverse[None, :]).astype(np.float32)
    angles = np.concatenate([angles, angles], axis=1).astype(np.float64)
    cosine = np.cos(angles).astype(np.float32)
    sine_table = np.sin(angles).astype(np.float32)
    return (jnp.asarray(cosine), jnp.asarray(sine_table))


def rotate(states, cosine, sine_table):
    halfway = states.shape[-1] // 2
    turned = jnp.concatenate([-states[..., halfway:], states[..., :halfway]], axis=-1)
    return states * cosine[None, :, None, :] + turned * sine_table[None, :, None, :]


def attend(query_heads, key_heads, value_heads, kv_count):
    members, length, head_count, head_size = query_heads.shape
    group_size = head_count // kv_count
    grouped = query_heads.reshape(members, length, kv_count, group_size, head_size)
    scores = jnp.einsum(
        "mskgd,mtkd->mkgst", grouped, key_heads, preferred_element_type=jnp.float32
    ) / math.sqrt(head_size)
    causal = jnp.arange(length)[None, :] <= jnp.arange(length)[:, None]
    scores = jnp.where(causal, scores, MASKED)
    top = jnp.max(scores, axis=-1, keepdims=True)
    weights = jnp.exp(scores - top)
    weights = (weights / jnp.sum(weights, axis=-1, keepdims=True)).astype(jnp.bfloat16)
    context = jnp.einsum(
        "mkgst,mtkd->mskgd", weights, value_heads, preferred_element_type=jnp.float32
    )
    return context.astype(jnp.bfloat16).reshape(members, length, head_count * head_size)


def on_device(
    token_ids,
    fit_ranks,
    embed_table,
    norm_gain,
    qkv_weight,
    qkv_bias,
    out_weight,
    value_weight,
    qkv_left,
    qkv_right,
    out_left,
    out_right,
):
    members, length = token_ids.shape
    row_count = members * length
    mp_size = lax.axis_size("mp")
    heads_here = HQ // mp_size
    kv_here = HK // mp_size
    member_count = lax.axis_size(MEMBER)
    population = members * member_count
    feature_rows = qkv_weight.shape[0]
    qkv_cols = qkv_weight.shape[1]
    out_cols = out_weight.shape[1]
    contract_rows = (((0,), (0,)), ((), ()))
    packed_ids = jnp.concatenate([token_ids, fit_ranks[:, None]], axis=1)
    spread_ids = jnp.broadcast_to(packed_ids[None], (member_count,) + packed_ids.shape)
    every_ids = lax.all_to_all(spread_ids, MEMBER, split_axis=0, concat_axis=0, tiled=True)
    all_ids = every_ids[:, :, :length].reshape(population, length)
    all_ranks = every_ids[:, :, length].reshape(population)
    stacked = jnp.concatenate(
        [
            jnp.concatenate([qkv_weight, out_weight], axis=1),
            jnp.concatenate([qkv_right, out_left], axis=1),
        ],
        axis=0,
    )
    y_count = lax.axis_size("y")
    spread_rows = jnp.broadcast_to(stacked[None], (y_count,) + stacked.shape)
    gathered = lax.all_to_all(spread_rows, "y", split_axis=0, concat_axis=0, tiled=True)
    gathered = lax.all_gather(gathered, BLOCK_AXES, axis=1)
    gathered = gathered.reshape((member_count,) + stacked.shape)
    block_qkv = gathered[:, :feature_rows, :qkv_cols]
    block_out = gathered[:, :feature_rows, qkv_cols:]
    right_cols = gathered[:, feature_rows:, :qkv_cols].reshape(population, qkv_cols)
    left_cols = gathered[:, feature_rows:, qkv_cols:].reshape(population, out_cols)
    mp_index = lax.axis_index("mp")
    share = members // mp_size
    half_ids = lax.dynamic_slice_in_dim(
        all_ids.reshape(member_count, members, length), mp_index * share, share, 1
    )
    picked = embed_table.at[:, half_ids.reshape(-1)].get(mode="promise_in_bounds")
    token_block = share * length
    factor_width = 2 * feature_rows * members
    factor_rows = -(-factor_width // token_block)
    factors = jnp.concatenate(
        [
            qkv_left.reshape(members, member_count, feature_rows),
            out_right.reshape(members, member_count, feature_rows),
        ],
        axis=2,
    )
    factors = factors.transpose(1, 0, 2).reshape(member_count, factor_width)
    factors = jnp.pad(factors, ((0, 0), (0, factor_rows * token_block - factor_width)))
    factors = factors.reshape(member_count, factor_rows, token_block).transpose(1, 0, 2)
    combined = jnp.concatenate([picked, factors.reshape(factor_rows, -1)], axis=0)
    arrived = lax.all_to_all(combined, MEMBER, split_axis=1, concat_axis=0, tiled=True)
    arrived = arrived.reshape(member_count, feature_rows + factor_rows, token_block)
    own_half = arrived[:, :feature_rows, :]
    factor_cols = arrived[:, feature_rows:, :].reshape(member_count, factor_rows * token_block)
    factor_cols = factor_cols[:, :factor_width].reshape(population, 2 * feature_rows)
    other_half = lax.ppermute(own_half, "mp", perm=[(0, 1), (1, 0)])
    embedded = jnp.where(
        mp_index == 0,
        jnp.concatenate([own_half, other_half], axis=2),
        jnp.concatenate([other_half, own_half], axis=2),
    )
    left_rows = factor_cols[:, :feature_rows]
    right_rows = factor_cols[:, feature_rows:]
    features = embedded.astype(jnp.float32)
    inverse_rms = lax.rsqrt(jnp.mean(features * features, axis=(0, 1), keepdims=True) + EPSILON)
    gain = norm_gain.reshape(member_count, feature_rows, 1)
    normed = (features * inverse_rms * gain).astype(jnp.bfloat16)
    base_proj = jnp.einsum("abt,abn->tn", normed, block_qkv, preferred_element_type=jnp.float32)
    normed_members = normed.reshape(member_count, feature_rows, members, length)
    left_blocks = qkv_left.reshape(members, member_count, feature_rows)
    coef_in = jnp.einsum(
        "abms,mab->ms", normed_members, left_blocks, preferred_element_type=jnp.float32
    )
    projected = (
        base_proj.reshape(members, length, -1)
        + SIGMA * coef_in[:, :, None] * qkv_right.astype(jnp.float32)[:, None, :]
        + qkv_bias[None, None, :]
    )
    query_width = heads_here * HD
    kv_width = kv_here * HD
    cosine, sine_table = rope_tables(length, HD)
    query_heads = rotate(
        projected[:, :, :query_width].reshape(members, length, heads_here, HD), cosine, sine_table
    ).astype(jnp.bfloat16)
    key_heads = rotate(
        projected[:, :, query_width : query_width + kv_width].reshape(members, length, kv_here, HD),
        cosine,
        sine_table,
    ).astype(jnp.bfloat16)
    value_heads = (
        projected[:, :, query_width + kv_width :]
        .reshape(members, length, kv_here, HD)
        .astype(jnp.bfloat16)
    )
    context = attend(query_heads, key_heads, value_heads, kv_here)
    coef_out = jnp.einsum("msq,mq->ms", context, out_left, preferred_element_type=jnp.float32)
    flat_context = context.reshape(row_count, query_width)
    partial_out = jnp.einsum(
        "tc,abc->abt", flat_context, block_out, preferred_element_type=jnp.float32
    )
    right_blocks = out_right.reshape(members, member_count, feature_rows).astype(jnp.float32)
    head_term = partial_out.reshape(member_count, feature_rows, members, length) + SIGMA * (
        right_blocks.transpose(1, 2, 0)[:, :, :, None] * coef_out[None, None, :, :]
    )
    head_term = head_term.reshape(member_count, feature_rows, mp_size, share * length)
    own_term = lax.dynamic_index_in_dim(head_term, mp_index, axis=2, keepdims=False)
    sent_term = lax.dynamic_index_in_dim(head_term, 1 - mp_index, axis=2, keepdims=False)
    got_term = lax.ppermute(sent_term.astype(jnp.bfloat16), "mp", perm=[(0, 1), (1, 0)])
    own_embed = own_half.astype(jnp.float32)
    residual = own_embed + own_term + got_term.astype(jnp.float32)
    inverse_out = lax.rsqrt(jnp.mean(residual * residual, axis=(0, 1), keepdims=True) + EPSILON)
    value_gain = value_weight.reshape(member_count, feature_rows, 1)
    value_rows = jnp.sum(residual * inverse_out * value_gain, axis=(0, 1)).reshape(share, length)
    rank_values = all_ranks.astype(jnp.float32)
    center = jnp.sum(rank_values) / population
    spread = jnp.sum(rank_values * rank_values) / population - center * center
    fitness = (rank_values - center) * lax.rsqrt(spread + EPSILON)
    weighted_in = left_rows.astype(jnp.float32) * fitness[:, None]
    qkv_grad = lax.dot_general(
        weighted_in,
        right_cols.astype(jnp.float32),
        contract_rows,
        precision=lax.Precision.HIGHEST,
        preferred_element_type=jnp.float32,
    ) / (population * SIGMA)
    weighted_out = right_rows.astype(jnp.float32) * fitness[:, None]
    out_grad = lax.dot_general(
        weighted_out,
        left_cols.astype(jnp.float32),
        contract_rows,
        precision=lax.Precision.HIGHEST,
        preferred_element_type=jnp.float32,
    ) / (population * SIGMA)
    return (value_rows, qkv_grad, out_grad)


def solution(mesh):
    member_size, mp_size = mesh.devices.shape
    chips = member_size // (2 * 4 * 4)
    split_mesh = jax.sharding.Mesh(
        mesh.devices.reshape(chips, 4, 4, 2, mp_size), ("y", "zl", "x", "c", "mp")
    )
    placed = (
        P(MEMBER, None),
        P(MEMBER),
        P(MEMBER, None),
        P(),
        P(MEMBER, "mp"),
        P("mp"),
        P(MEMBER, "mp"),
        P(),
        P(MEMBER, None),
        P(MEMBER, "mp"),
        P(MEMBER, "mp"),
        P(MEMBER, None),
    )
    return jax.shard_map(
        on_device,
        mesh=split_mesh,
        in_specs=placed,
        out_specs=(P(MEMBER + ("mp",), None), P(MEMBER, "mp"), P(MEMBER, "mp")),
        check_vma=False,
    )
```

```python
import math

import jax
import numpy as np
import jax.numpy as jnp
from jax import lax
from jax.sharding import PartitionSpec as P

HD = 128
HQ = 14
HK = 2


SIGMA = 0.01
EPSILON = 1e-06
THETA = 1000000.0
MASKED = -1e30
MEMBER = ("y", "zl", "x", "c")
BLOCK_AXES = ("zl", "x", "c")


def rope_tables(length, head_size):
    halfway = head_size // 2
    steps = np.arange(halfway, dtype=np.float32) * np.float32(2.0) / np.float32(head_size)
    inverse = np.power(np.float32(THETA), -steps).astype(np.float32)
    places = np.arange(length, dtype=np.float32)
    angles = (places[:, None] * inverse[None, :]).astype(np.float32)
    angles = np.concatenate([angles, angles], axis=1).astype(np.float64)
    cosine = np.cos(angles).astype(np.float32)
    sine_table = np.sin(angles).astype(np.float32)
    return (jnp.asarray(cosine), jnp.asarray(sine_table))


def rotate(states, cosine, sine_table):
    halfway = states.shape[-1] // 2
    turned = jnp.concatenate([-states[..., halfway:], states[..., :halfway]], axis=-1)
    return states * cosine[None, :, None, :] + turned * sine_table[None, :, None, :]


def attend(query_heads, key_heads, value_heads, kv_count):
    members, length, head_count, head_size = query_heads.shape
    group_size = head_count // kv_count
    grouped = query_heads.reshape(members, length, kv_count, group_size, head_size)
    scores = jnp.einsum(
        "mskgd,mtkd->mkgst", grouped, key_heads, preferred_element_type=jnp.float32
    ) / math.sqrt(head_size)
    causal = jnp.arange(length)[None, :] <= jnp.arange(length)[:, None]
    scores = jnp.where(causal, scores, MASKED)
    top = jnp.max(scores, axis=-1, keepdims=True)
    weights = jnp.exp(scores - top)
    weights = (weights / jnp.sum(weights, axis=-1, keepdims=True)).astype(jnp.bfloat16)
    context = jnp.einsum(
        "mkgst,mtkd->mskgd", weights, value_heads, preferred_element_type=jnp.float32
    )
    return context.astype(jnp.bfloat16).reshape(members, length, head_count * head_size)


def on_device(
    token_ids,
    fit_ranks,
    embed_table,
    norm_gain,
    qkv_weight,
    qkv_bias,
    out_weight,
    value_weight,
    qkv_left,
    qkv_right,
    out_left,
    out_right,
):
    members, length = token_ids.shape
    row_count = members * length
    mp_size = lax.axis_size("mp")
    heads_here = HQ // mp_size
    kv_here = HK // mp_size
    member_count = lax.axis_size(MEMBER)
    population = members * member_count
    feature_rows = qkv_weight.shape[0]
    qkv_cols = qkv_weight.shape[1]
    out_cols = out_weight.shape[1]
    contract_rows = (((0,), (0,)), ((), ()))
    packed_ids = jnp.concatenate([token_ids, fit_ranks[:, None]], axis=1)
    spread_ids = jnp.broadcast_to(packed_ids[None], (member_count,) + packed_ids.shape)
    every_ids = lax.all_to_all(spread_ids, MEMBER, split_axis=0, concat_axis=0, tiled=True)
    all_ids = every_ids[:, :, :length].reshape(population, length)
    all_ranks = every_ids[:, :, length].reshape(population)
    stacked = jnp.concatenate(
        [
            jnp.concatenate([qkv_weight, out_weight], axis=1),
            jnp.concatenate([qkv_right, out_left], axis=1),
        ],
        axis=0,
    )
    block_gathered = lax.all_gather(stacked, BLOCK_AXES, axis=0)
    mp_index = lax.axis_index("mp")
    share = members // mp_size
    half_ids = lax.dynamic_slice_in_dim(
        all_ids.reshape(member_count, members, length), mp_index * share, share, 1
    )
    picked = embed_table.at[:, half_ids.reshape(-1)].get(mode="promise_in_bounds")
    after_pick = picked[0, 0] * jnp.zeros((), picked.dtype)
    gathered = lax.all_gather(block_gathered + after_pick, "y", axis=0)
    gathered = gathered.reshape((member_count,) + stacked.shape)
    block_qkv = gathered[:, :feature_rows, :qkv_cols]
    block_out = gathered[:, :feature_rows, qkv_cols:]
    right_cols = gathered[:, feature_rows:, :qkv_cols].reshape(population, qkv_cols)
    left_cols = gathered[:, feature_rows:, qkv_cols:].reshape(population, out_cols)
    token_block = share * length
    factor_width = 2 * feature_rows * members
    factor_rows = -(-factor_width // token_block)
    factors = jnp.concatenate(
        [
            qkv_left.reshape(members, member_count, feature_rows),
            out_right.reshape(members, member_count, feature_rows),
        ],
        axis=2,
    )
    factors = factors.transpose(1, 0, 2).reshape(member_count, factor_width)
    factors = jnp.pad(factors, ((0, 0), (0, factor_rows * token_block - factor_width)))
    factors = factors.reshape(member_count, factor_rows, token_block).transpose(1, 0, 2)
    combined = jnp.concatenate([picked, factors.reshape(factor_rows, -1)], axis=0)
    arrived = lax.all_to_all(combined, MEMBER, split_axis=1, concat_axis=0, tiled=True)
    arrived = arrived.reshape(member_count, feature_rows + factor_rows, token_block)
    own_half = arrived[:, :feature_rows, :]
    factor_cols = arrived[:, feature_rows:, :].reshape(member_count, factor_rows * token_block)
    factor_cols = factor_cols[:, :factor_width].reshape(population, 2 * feature_rows)
    other_half = lax.ppermute(own_half, "mp", perm=[(0, 1), (1, 0)])
    embedded = jnp.where(
        mp_index == 0,
        jnp.concatenate([own_half, other_half], axis=2),
        jnp.concatenate([other_half, own_half], axis=2),
    )
    left_rows = factor_cols[:, :feature_rows]
    right_rows = factor_cols[:, feature_rows:]
    features = embedded.astype(jnp.float32)
    inverse_rms = lax.rsqrt(jnp.mean(features * features, axis=(0, 1), keepdims=True) + EPSILON)
    gain = norm_gain.reshape(member_count, feature_rows, 1)
    normed = (features * inverse_rms * gain).astype(jnp.bfloat16)
    base_proj = jnp.einsum("abt,abn->tn", normed, block_qkv, preferred_element_type=jnp.float32)
    normed_members = normed.reshape(member_count, feature_rows, members, length)
    left_blocks = qkv_left.reshape(members, member_count, feature_rows)
    coef_in = jnp.einsum(
        "abms,mab->ms", normed_members, left_blocks, preferred_element_type=jnp.float32
    )
    projected = (
        base_proj.reshape(members, length, -1)
        + SIGMA * coef_in[:, :, None] * qkv_right.astype(jnp.float32)[:, None, :]
        + qkv_bias[None, None, :]
    )
    query_width = heads_here * HD
    kv_width = kv_here * HD
    cosine, sine_table = rope_tables(length, HD)
    query_heads = rotate(
        projected[:, :, :query_width].reshape(members, length, heads_here, HD), cosine, sine_table
    ).astype(jnp.bfloat16)
    key_heads = rotate(
        projected[:, :, query_width : query_width + kv_width].reshape(members, length, kv_here, HD),
        cosine,
        sine_table,
    ).astype(jnp.bfloat16)
    value_heads = (
        projected[:, :, query_width + kv_width :]
        .reshape(members, length, kv_here, HD)
        .astype(jnp.bfloat16)
    )
    context = attend(query_heads, key_heads, value_heads, kv_here)
    coef_out = jnp.einsum("msq,mq->ms", context, out_left, preferred_element_type=jnp.float32)
    flat_context = context.reshape(row_count, query_width)
    partial_out = jnp.einsum(
        "tc,abc->abt", flat_context, block_out, preferred_element_type=jnp.float32
    )
    right_blocks = out_right.reshape(members, member_count, feature_rows).astype(jnp.float32)
    head_term = partial_out.reshape(member_count, feature_rows, members, length) + SIGMA * (
        right_blocks.transpose(1, 2, 0)[:, :, :, None] * coef_out[None, None, :, :]
    )
    head_term = head_term.reshape(member_count, feature_rows, mp_size, share * length)
    own_term = lax.dynamic_index_in_dim(head_term, mp_index, axis=2, keepdims=False)
    sent_term = lax.dynamic_index_in_dim(head_term, 1 - mp_index, axis=2, keepdims=False)
    got_term = lax.ppermute(sent_term.astype(jnp.bfloat16), "mp", perm=[(0, 1), (1, 0)])
    own_embed = own_half.astype(jnp.float32)
    residual = own_embed + own_term + got_term.astype(jnp.float32)
    inverse_out = lax.rsqrt(jnp.mean(residual * residual, axis=(0, 1), keepdims=True) + EPSILON)
    value_gain = value_weight.reshape(member_count, feature_rows, 1)
    value_rows = jnp.sum(residual * inverse_out * value_gain, axis=(0, 1)).reshape(share, length)
    rank_values = all_ranks.astype(jnp.float32)
    center = jnp.sum(rank_values) / population
    spread = jnp.sum(rank_values * rank_values) / population - center * center
    fitness = (rank_values - center) * lax.rsqrt(spread + EPSILON)
    weighted_in = left_rows.astype(jnp.float32) * fitness[:, None]
    qkv_grad = lax.dot_general(
        weighted_in,
        right_cols.astype(jnp.float32),
        contract_rows,
        precision=lax.Precision.HIGHEST,
        preferred_element_type=jnp.float32,
    ) / (population * SIGMA)
    weighted_out = right_rows.astype(jnp.float32) * fitness[:, None]
    out_grad = lax.dot_general(
        weighted_out,
        left_cols.astype(jnp.float32),
        contract_rows,
        precision=lax.Precision.HIGHEST,
        preferred_element_type=jnp.float32,
    ) / (population * SIGMA)
    return (value_rows, qkv_grad, out_grad)


def solution(mesh):
    member_size, mp_size = mesh.devices.shape
    chips = member_size // (2 * 4 * 4)
    split_mesh = jax.sharding.Mesh(
        mesh.devices.reshape(chips, 4, 4, 2, mp_size), ("y", "zl", "x", "c", "mp")
    )
    placed = (
        P(MEMBER, None),
        P(MEMBER),
        P(MEMBER, None),
        P(),
        P(MEMBER, "mp"),
        P("mp"),
        P(MEMBER, "mp"),
        P(),
        P(MEMBER, None),
        P(MEMBER, "mp"),
        P(MEMBER, "mp"),
        P(MEMBER, None),
    )
    return jax.shard_map(
        on_device,
        mesh=split_mesh,
        in_specs=placed,
        out_specs=(P(MEMBER + ("mp",), None), P(MEMBER, "mp"), P(MEMBER, "mp")),
        check_vma=False,
    )
```

```python
import math

import jax
import numpy as np
import jax.numpy as jnp
from jax import lax
from jax.sharding import PartitionSpec as P

HD = 128
HQ = 14
HK = 2


SIGMA = 0.01
EPSILON = 1e-06
THETA = 1000000.0
MASKED = -1e30
MEMBER = ("y", "zl", "x", "c")
BLOCK_AXES = ("zl", "x", "c")


def rope_tables(length, head_size):
    halfway = head_size // 2
    steps = np.arange(halfway, dtype=np.float32) * np.float32(2.0) / np.float32(head_size)
    inverse = np.power(np.float32(THETA), -steps).astype(np.float32)
    places = np.arange(length, dtype=np.float32)
    angles = (places[:, None] * inverse[None, :]).astype(np.float32)
    angles = np.concatenate([angles, angles], axis=1).astype(np.float64)
    cosine = np.cos(angles).astype(np.float32)
    sine_table = np.sin(angles).astype(np.float32)
    return (jnp.asarray(cosine), jnp.asarray(sine_table))


def rotate(states, cosine, sine_table):
    halfway = states.shape[-1] // 2
    turned = jnp.concatenate([-states[..., halfway:], states[..., :halfway]], axis=-1)
    return states * cosine[None, :, None, :] + turned * sine_table[None, :, None, :]


def attend(query_heads, key_heads, value_heads, kv_count):
    members, length, head_count, head_size = query_heads.shape
    group_size = head_count // kv_count
    grouped = query_heads.reshape(members, length, kv_count, group_size, head_size)
    scores = jnp.einsum(
        "mskgd,mtkd->mkgst", grouped, key_heads, preferred_element_type=jnp.float32
    ) / math.sqrt(head_size)
    causal = jnp.arange(length)[None, :] <= jnp.arange(length)[:, None]
    scores = jnp.where(causal, scores, MASKED)
    top = jnp.max(scores, axis=-1, keepdims=True)
    weights = jnp.exp(scores - top)
    weights = (weights / jnp.sum(weights, axis=-1, keepdims=True)).astype(jnp.bfloat16)
    context = jnp.einsum(
        "mkgst,mtkd->mskgd", weights, value_heads, preferred_element_type=jnp.float32
    )
    return context.astype(jnp.bfloat16).reshape(members, length, head_count * head_size)


def on_device(
    token_ids,
    fit_ranks,
    embed_table,
    norm_gain,
    qkv_weight,
    qkv_bias,
    out_weight,
    value_weight,
    qkv_left,
    qkv_right,
    out_left,
    out_right,
):
    members, length = token_ids.shape
    row_count = members * length
    mp_size = lax.axis_size("mp")
    heads_here = HQ // mp_size
    kv_here = HK // mp_size
    member_count = lax.axis_size(MEMBER)
    population = members * member_count
    feature_rows = qkv_weight.shape[0]
    qkv_cols = qkv_weight.shape[1]
    out_cols = out_weight.shape[1]
    contract_rows = (((0,), (0,)), ((), ()))
    packed_ids = jnp.concatenate([token_ids, fit_ranks[:, None]], axis=1)
    spread_ids = jnp.broadcast_to(packed_ids[None], (member_count,) + packed_ids.shape)
    every_ids = lax.all_to_all(spread_ids, MEMBER, split_axis=0, concat_axis=0, tiled=True)
    all_ids = every_ids[:, :, :length].reshape(population, length)
    all_ranks = every_ids[:, :, length].reshape(population)
    stacked = jnp.concatenate(
        [
            jnp.concatenate([qkv_weight, out_weight], axis=1),
            jnp.concatenate([qkv_right, out_left], axis=1),
        ],
        axis=0,
    )
    y_count = lax.axis_size("y")
    spread_rows = jnp.broadcast_to(stacked[None], (y_count,) + stacked.shape)
    gathered = lax.all_to_all(spread_rows, "y", split_axis=0, concat_axis=0, tiled=True)
    gathered = lax.all_gather(gathered, BLOCK_AXES, axis=1)
    gathered = gathered.reshape((member_count,) + stacked.shape)
    block_qkv = gathered[:, :feature_rows, :qkv_cols]
    block_out = gathered[:, :feature_rows, qkv_cols:]
    right_cols = gathered[:, feature_rows:, :qkv_cols].reshape(population, qkv_cols)
    left_cols = gathered[:, feature_rows:, qkv_cols:].reshape(population, out_cols)
    mp_index = lax.axis_index("mp")
    share = members // mp_size
    half_ids = lax.dynamic_slice_in_dim(
        all_ids.reshape(member_count, members, length), mp_index * share, share, 1
    )
    picked = embed_table.at[:, half_ids.reshape(-1)].get(mode="promise_in_bounds")
    token_block = share * length
    factor_width = 2 * feature_rows * members
    factor_rows = -(-factor_width // token_block)
    factors = jnp.concatenate(
        [
            qkv_left.reshape(members, member_count, feature_rows),
            out_right.reshape(members, member_count, feature_rows),
        ],
        axis=2,
    )
    factors = factors.transpose(1, 0, 2).reshape(member_count, factor_width)
    factors = jnp.pad(factors, ((0, 0), (0, factor_rows * token_block - factor_width)))
    factors = factors.reshape(member_count, factor_rows, token_block).transpose(1, 0, 2)
    combined = jnp.concatenate([picked, factors.reshape(factor_rows, -1)], axis=0)
    carried = feature_rows + factor_rows
    doubled = jnp.broadcast_to(
        combined.reshape(carried, member_count, 1, token_block),
        (carried, member_count, mp_size, token_block),
    ).reshape(carried, -1)
    arrived = lax.all_to_all(doubled, MEMBER + ("mp",), split_axis=1, concat_axis=0, tiled=True)
    arrived = arrived.reshape(member_count, mp_size, carried, token_block)
    own_half = lax.dynamic_index_in_dim(arrived, mp_index, axis=1, keepdims=False)[:, :feature_rows]
    factor_cols = arrived[:, 0, feature_rows:, :].reshape(member_count, factor_rows * token_block)
    factor_cols = factor_cols[:, :factor_width].reshape(population, 2 * feature_rows)
    embedded = arrived[:, :, :feature_rows, :].transpose(0, 2, 1, 3).reshape(
        member_count, feature_rows, mp_size * token_block
    )
    left_rows = factor_cols[:, :feature_rows]
    right_rows = factor_cols[:, feature_rows:]
    features = embedded.astype(jnp.float32)
    inverse_rms = lax.rsqrt(jnp.mean(features * features, axis=(0, 1), keepdims=True) + EPSILON)
    gain = norm_gain.reshape(member_count, feature_rows, 1)
    normed = (features * inverse_rms * gain).astype(jnp.bfloat16)
    base_proj = jnp.einsum("abt,abn->tn", normed, block_qkv, preferred_element_type=jnp.float32)
    normed_members = normed.reshape(member_count, feature_rows, members, length)
    left_blocks = qkv_left.reshape(members, member_count, feature_rows)
    coef_in = jnp.einsum(
        "abms,mab->ms", normed_members, left_blocks, preferred_element_type=jnp.float32
    )
    projected = (
        base_proj.reshape(members, length, -1)
        + SIGMA * coef_in[:, :, None] * qkv_right.astype(jnp.float32)[:, None, :]
        + qkv_bias[None, None, :]
    )
    query_width = heads_here * HD
    kv_width = kv_here * HD
    cosine, sine_table = rope_tables(length, HD)
    query_heads = rotate(
        projected[:, :, :query_width].reshape(members, length, heads_here, HD), cosine, sine_table
    ).astype(jnp.bfloat16)
    key_heads = rotate(
        projected[:, :, query_width : query_width + kv_width].reshape(members, length, kv_here, HD),
        cosine,
        sine_table,
    ).astype(jnp.bfloat16)
    value_heads = (
        projected[:, :, query_width + kv_width :]
        .reshape(members, length, kv_here, HD)
        .astype(jnp.bfloat16)
    )
    context = attend(query_heads, key_heads, value_heads, kv_here)
    coef_out = jnp.einsum("msq,mq->ms", context, out_left, preferred_element_type=jnp.float32)
    flat_context = context.reshape(row_count, query_width)
    partial_out = jnp.einsum(
        "tc,abc->abt", flat_context, block_out, preferred_element_type=jnp.float32
    )
    right_blocks = out_right.reshape(members, member_count, feature_rows).astype(jnp.float32)
    head_term = partial_out.reshape(member_count, feature_rows, members, length) + SIGMA * (
        right_blocks.transpose(1, 2, 0)[:, :, :, None] * coef_out[None, None, :, :]
    )
    head_term = head_term.reshape(member_count, feature_rows, mp_size, share * length)
    own_term = lax.dynamic_index_in_dim(head_term, mp_index, axis=2, keepdims=False)
    sent_term = lax.dynamic_index_in_dim(head_term, 1 - mp_index, axis=2, keepdims=False)
    got_term = lax.ppermute(sent_term.astype(jnp.bfloat16), "mp", perm=[(0, 1), (1, 0)])
    own_embed = own_half.astype(jnp.float32)
    residual = own_embed + own_term + got_term.astype(jnp.float32)
    inverse_out = lax.rsqrt(jnp.mean(residual * residual, axis=(0, 1), keepdims=True) + EPSILON)
    value_gain = value_weight.reshape(member_count, feature_rows, 1)
    value_rows = jnp.sum(residual * inverse_out * value_gain, axis=(0, 1)).reshape(share, length)
    rank_values = all_ranks.astype(jnp.float32)
    center = jnp.sum(rank_values) / population
    spread = jnp.sum(rank_values * rank_values) / population - center * center
    fitness = (rank_values - center) * lax.rsqrt(spread + EPSILON)
    weighted_in = left_rows.astype(jnp.float32) * fitness[:, None]
    qkv_grad = lax.dot_general(
        weighted_in,
        right_cols.astype(jnp.float32),
        contract_rows,
        precision=lax.Precision.HIGHEST,
        preferred_element_type=jnp.float32,
    ) / (population * SIGMA)
    weighted_out = right_rows.astype(jnp.float32) * fitness[:, None]
    out_grad = lax.dot_general(
        weighted_out,
        left_cols.astype(jnp.float32),
        contract_rows,
        precision=lax.Precision.HIGHEST,
        preferred_element_type=jnp.float32,
    ) / (population * SIGMA)
    return (value_rows, qkv_grad, out_grad)


def solution(mesh):
    member_size, mp_size = mesh.devices.shape
    chips = member_size // (2 * 4 * 4)
    split_mesh = jax.sharding.Mesh(
        mesh.devices.reshape(chips, 4, 4, 2, mp_size), ("y", "zl", "x", "c", "mp")
    )
    placed = (
        P(MEMBER, None),
        P(MEMBER),
        P(MEMBER, None),
        P(),
        P(MEMBER, "mp"),
        P("mp"),
        P(MEMBER, "mp"),
        P(),
        P(MEMBER, None),
        P(MEMBER, "mp"),
        P(MEMBER, "mp"),
        P(MEMBER, None),
    )
    return jax.shard_map(
        on_device,
        mesh=split_mesh,
        in_specs=placed,
        out_specs=(P(MEMBER + ("mp",), None), P(MEMBER, "mp"), P(MEMBER, "mp")),
        check_vma=False,
    )
```

```python
import math

import jax
import numpy as np
import jax.numpy as jnp
from jax import lax
from jax.sharding import PartitionSpec as P

HD = 128
HQ = 14
HK = 2


SIGMA = 0.01
EPSILON = 1e-06
THETA = 1000000.0
MASKED = -1e30
MEMBER = ("y", "zl", "x", "c")
BLOCK_AXES = ("zl", "x", "c")


def rope_tables(length, head_size):
    halfway = head_size // 2
    steps = np.arange(halfway, dtype=np.float32) * np.float32(2.0) / np.float32(head_size)
    inverse = np.power(np.float32(THETA), -steps).astype(np.float32)
    places = np.arange(length, dtype=np.float32)
    angles = (places[:, None] * inverse[None, :]).astype(np.float32)
    angles = np.concatenate([angles, angles], axis=1).astype(np.float64)
    cosine = np.cos(angles).astype(np.float32)
    sine_table = np.sin(angles).astype(np.float32)
    return (jnp.asarray(cosine), jnp.asarray(sine_table))


def rotate(states, cosine, sine_table):
    halfway = states.shape[-1] // 2
    turned = jnp.concatenate([-states[..., halfway:], states[..., :halfway]], axis=-1)
    return states * cosine[None, :, None, :] + turned * sine_table[None, :, None, :]


def attend(query_heads, key_heads, value_heads, kv_count):
    members, length, head_count, head_size = query_heads.shape
    group_size = head_count // kv_count
    grouped = query_heads.reshape(members, length, kv_count, group_size, head_size)
    scores = jnp.einsum(
        "mskgd,mtkd->mkgst", grouped, key_heads, preferred_element_type=jnp.float32
    ) / math.sqrt(head_size)
    causal = jnp.arange(length)[None, :] <= jnp.arange(length)[:, None]
    scores = jnp.where(causal, scores, MASKED)
    top = jnp.max(scores, axis=-1, keepdims=True)
    weights = jnp.exp(scores - top)
    weights = (weights / jnp.sum(weights, axis=-1, keepdims=True)).astype(jnp.bfloat16)
    context = jnp.einsum(
        "mkgst,mtkd->mskgd", weights, value_heads, preferred_element_type=jnp.float32
    )
    return context.astype(jnp.bfloat16).reshape(members, length, head_count * head_size)


def on_device(
    token_ids,
    fit_ranks,
    embed_table,
    norm_gain,
    qkv_weight,
    qkv_bias,
    out_weight,
    value_weight,
    qkv_left,
    qkv_right,
    out_left,
    out_right,
):
    members, length = token_ids.shape
    row_count = members * length
    mp_size = lax.axis_size("mp")
    heads_here = HQ // mp_size
    kv_here = HK // mp_size
    member_count = lax.axis_size(MEMBER)
    population = members * member_count
    feature_rows = qkv_weight.shape[0]
    qkv_cols = qkv_weight.shape[1]
    out_cols = out_weight.shape[1]
    contract_rows = (((0,), (0,)), ((), ()))
    packed_ids = jnp.concatenate([token_ids, fit_ranks[:, None]], axis=1)
    spread_ids = jnp.broadcast_to(packed_ids[None], (member_count,) + packed_ids.shape)
    every_ids = lax.all_to_all(spread_ids, MEMBER, split_axis=0, concat_axis=0, tiled=True)
    all_ids = every_ids[:, :, :length].reshape(population, length)
    all_ranks = every_ids[:, :, length].reshape(population)
    stacked = jnp.concatenate(
        [
            jnp.concatenate([qkv_weight, out_weight], axis=1),
            jnp.concatenate([qkv_right, out_left], axis=1),
        ],
        axis=0,
    )
    y_count = lax.axis_size("y")
    spread_rows = jnp.broadcast_to(stacked[None], (y_count,) + stacked.shape)
    gathered = lax.all_to_all(spread_rows, "y", split_axis=0, concat_axis=0, tiled=True)
    gathered = lax.all_gather(gathered, BLOCK_AXES, axis=1)
    gathered = gathered.reshape((member_count,) + stacked.shape)
    block_qkv = gathered[:, :feature_rows, :qkv_cols]
    block_out = gathered[:, :feature_rows, qkv_cols:]
    right_cols = gathered[:, feature_rows:, :qkv_cols].reshape(population, qkv_cols)
    left_cols = gathered[:, feature_rows:, qkv_cols:].reshape(population, out_cols)
    mp_index = lax.axis_index("mp")
    share = members // mp_size
    half_ids = lax.dynamic_slice_in_dim(
        all_ids.reshape(member_count, members, length), mp_index * share, share, 1
    )
    picked = embed_table.at[:, half_ids.reshape(-1)].get(mode="promise_in_bounds")
    token_block = share * length
    factor_width = 2 * feature_rows * members
    factor_rows = -(-factor_width // token_block)
    factors = jnp.concatenate(
        [
            qkv_left.reshape(members, member_count, feature_rows),
            out_right.reshape(members, member_count, feature_rows),
        ],
        axis=2,
    )
    factors = factors.transpose(1, 0, 2).reshape(member_count, factor_width)
    factors = jnp.pad(factors, ((0, 0), (0, factor_rows * token_block - factor_width)))
    factors = factors.reshape(member_count, factor_rows, token_block).transpose(1, 0, 2)
    combined = jnp.concatenate([picked, factors.reshape(factor_rows, -1)], axis=0)
    arrived = lax.all_to_all(combined, MEMBER, split_axis=1, concat_axis=0, tiled=True)
    arrived = arrived.reshape(member_count, feature_rows + factor_rows, token_block)
    own_half = arrived[:, :feature_rows, :]
    factor_cols = arrived[:, feature_rows:, :].reshape(member_count, factor_rows * token_block)
    factor_cols = factor_cols[:, :factor_width].reshape(population, 2 * feature_rows)
    weights_ready = gathered[0, 0, 0] * jnp.zeros((), gathered.dtype)
    other_half = lax.ppermute(own_half + weights_ready, "mp", perm=[(0, 1), (1, 0)])
    embedded = jnp.where(
        mp_index == 0,
        jnp.concatenate([own_half, other_half], axis=2),
        jnp.concatenate([other_half, own_half], axis=2),
    )
    left_rows = factor_cols[:, :feature_rows]
    right_rows = factor_cols[:, feature_rows:]
    features = embedded.astype(jnp.float32)
    inverse_rms = lax.rsqrt(jnp.mean(features * features, axis=(0, 1), keepdims=True) + EPSILON)
    gain = norm_gain.reshape(member_count, feature_rows, 1)
    normed = (features * inverse_rms * gain).astype(jnp.bfloat16)
    base_proj = jnp.einsum("abt,abn->tn", normed, block_qkv, preferred_element_type=jnp.float32)
    normed_members = normed.reshape(member_count, feature_rows, members, length)
    left_blocks = qkv_left.reshape(members, member_count, feature_rows)
    coef_in = jnp.einsum(
        "abms,mab->ms", normed_members, left_blocks, preferred_element_type=jnp.float32
    )
    projected = (
        base_proj.reshape(members, length, -1)
        + SIGMA * coef_in[:, :, None] * qkv_right.astype(jnp.float32)[:, None, :]
        + qkv_bias[None, None, :]
    )
    query_width = heads_here * HD
    kv_width = kv_here * HD
    cosine, sine_table = rope_tables(length, HD)
    query_heads = rotate(
        projected[:, :, :query_width].reshape(members, length, heads_here, HD), cosine, sine_table
    ).astype(jnp.bfloat16)
    key_heads = rotate(
        projected[:, :, query_width : query_width + kv_width].reshape(members, length, kv_here, HD),
        cosine,
        sine_table,
    ).astype(jnp.bfloat16)
    value_heads = (
        projected[:, :, query_width + kv_width :]
        .reshape(members, length, kv_here, HD)
        .astype(jnp.bfloat16)
    )
    context = attend(query_heads, key_heads, value_heads, kv_here)
    coef_out = jnp.einsum("msq,mq->ms", context, out_left, preferred_element_type=jnp.float32)
    flat_context = context.reshape(row_count, query_width)
    partial_out = jnp.einsum(
        "tc,abc->abt", flat_context, block_out, preferred_element_type=jnp.float32
    )
    right_blocks = out_right.reshape(members, member_count, feature_rows).astype(jnp.float32)
    head_term = partial_out.reshape(member_count, feature_rows, members, length) + SIGMA * (
        right_blocks.transpose(1, 2, 0)[:, :, :, None] * coef_out[None, None, :, :]
    )
    head_term = head_term.reshape(member_count, feature_rows, mp_size, share * length)
    own_term = lax.dynamic_index_in_dim(head_term, mp_index, axis=2, keepdims=False)
    sent_term = lax.dynamic_index_in_dim(head_term, 1 - mp_index, axis=2, keepdims=False)
    got_term = lax.ppermute(sent_term.astype(jnp.bfloat16), "mp", perm=[(0, 1), (1, 0)])
    own_embed = own_half.astype(jnp.float32)
    residual = own_embed + own_term + got_term.astype(jnp.float32)
    inverse_out = lax.rsqrt(jnp.mean(residual * residual, axis=(0, 1), keepdims=True) + EPSILON)
    value_gain = value_weight.reshape(member_count, feature_rows, 1)
    value_rows = jnp.sum(residual * inverse_out * value_gain, axis=(0, 1)).reshape(share, length)
    rank_values = all_ranks.astype(jnp.float32)
    center = jnp.sum(rank_values) / population
    spread = jnp.sum(rank_values * rank_values) / population - center * center
    fitness = (rank_values - center) * lax.rsqrt(spread + EPSILON)
    weighted_in = left_rows.astype(jnp.float32) * fitness[:, None]
    qkv_grad = lax.dot_general(
        weighted_in,
        right_cols.astype(jnp.float32),
        contract_rows,
        precision=lax.Precision.HIGHEST,
        preferred_element_type=jnp.float32,
    ) / (population * SIGMA)
    weighted_out = right_rows.astype(jnp.float32) * fitness[:, None]
    out_grad = lax.dot_general(
        weighted_out,
        left_cols.astype(jnp.float32),
        contract_rows,
        precision=lax.Precision.HIGHEST,
        preferred_element_type=jnp.float32,
    ) / (population * SIGMA)
    return (value_rows, qkv_grad, out_grad)


def solution(mesh):
    member_size, mp_size = mesh.devices.shape
    chips = member_size // (2 * 4 * 4)
    split_mesh = jax.sharding.Mesh(
        mesh.devices.reshape(chips, 4, 4, 2, mp_size), ("y", "zl", "x", "c", "mp")
    )
    placed = (
        P(MEMBER, None),
        P(MEMBER),
        P(MEMBER, None),
        P(),
        P(MEMBER, "mp"),
        P("mp"),
        P(MEMBER, "mp"),
        P(),
        P(MEMBER, None),
        P(MEMBER, "mp"),
        P(MEMBER, "mp"),
        P(MEMBER, None),
    )
    return jax.shard_map(
        on_device,
        mesh=split_mesh,
        in_specs=placed,
        out_specs=(P(MEMBER + ("mp",), None), P(MEMBER, "mp"), P(MEMBER, "mp")),
        check_vma=False,
    )
```
